512 devices in a mesh: dp: 16 (over z, core), expert: 32 (over x, y).
Axes of the slice: x: 4, y: 8, z: 8, core: 2. Of those that a mesh axis runs over, the one named last changes fastest.
Arguments:
- residual_in: bfloat16 [16384, 2048], P(('dp', 'expert')), may hold values from -6 to 6
- attention_out: bfloat16 [16384, 2048], P(('dp', 'expert')), may hold values from -6 to 6
- out_weight: bfloat16 [2048, 2048], P(None, 'dp'), may hold values from -0.125 to 0.125
- post_gain: float32 [2048], replicated, may hold values from 0.1 to 1.9
- router_weight: bfloat16 [2048, 32], replicated, may hold values from -0.125 to 0.125
- expert_ids: int32 [16384, 6], P(('dp', 'expert')), may hold values from 0 to 31, all different within a row; in each aligned block of 32 rows (0 to 31, 32 to 63, ...) at most 12 rows name the same one
- expert_slot: int32 [32], replicated, may hold values from 0 to 31, each once
- expert_gate_up: bfloat16 [32, 2048, 1408], P('expert', 'dp'), may hold values from -0.125 to 0.125
- expert_down: bfloat16 [32, 704, 2048], P('expert', None, 'dp'), may hold values from -0.21875 to 0.21875
- shared_gate_up: bfloat16 [2048, 2, 2816], P(None, None, 'dp'), may hold values from -0.125 to 0.125
- shared_down: bfloat16 [2816, 2048], P(None, 'dp'), may hold values from -0.109375 to 0.109375
- final_gain: float32 [2048], replicated, may hold values from 0.1 to 1.9
Outputs:
- mixed: bfloat16 [16384, 2048], P(('dp', 'expert'))
The draws below stay inside these ranges and needn't reach their ends.
Inputs may be any that keep to these rules, and one draw needn't show every extreme that they name: `expert_ids`: each row names 6 different experts. In each aligned block of 32 rows (the rows of one device) no expert is named by more than 12 rows, a bound that some block reaches. A permutation: expert e is held in slot expert_slot[e].
All inputs are finite; a program needn't handle non-finite values.
Results may differ from the reference program's by a relative error of at most 0.0069.
Values may be sent and summed in bfloat16 or wider, within the bound.
No kernel may reach another device: no remote copies, remote signals or barrier semaphores. Data moves between devices by JAX's collectives and lax.ppermute only.
A program may use at most 64 MiB of HBM per device.

```python
import math
import jax
import jax.numpy as jnp
import numpy as np
from jax import lax

D = 2048
HD = 2048
F = 704
FS = 2816
TOPK = 6
ROW_DEV = 32
EXPERTS = 32
ROW_BLOCKS = 512
ROWS = 16384
CAP = 12


def level_of(key, extent, cuts, low, largest):
    factor_of, own = 1.0, jax.random.fold_in(key, 6)
    for dim, parts in cuts:
        heights = jnp.exp(jax.random.uniform(jax.random.fold_in(own, dim), (parts,), jnp.float32, low / len(cuts), largest / len(cuts)))
        factor_of = factor_of * jnp.repeat(heights, extent[dim] // parts).reshape([-1 if axis == dim else 1 for axis in range(len(extent))])
    return factor_of


def deal_out(stream_key, own, number, rows, amount, top, bound, lean):
    order = jax.random.permutation(stream_key, amount)
    packed, ordinary = portions_of(amount, rows * top, bound, lean, True), portions_of(amount, rows * top, bound, lean, False)
    places = jnp.arange(amount)

    def named(tallies, offset_by):
        used = int((tallies > 0).sum())
        fixed = max(1, used // 4)
        passed = fixed + (places - fixed + offset_by * (used - fixed)) % max(1, amount - fixed)
        return jnp.zeros((amount,), jnp.int32).at[order[jnp.where(places < fixed, places, passed)]].set(jnp.asarray(tallies, jnp.int32))

    tallies = jnp.where(number % 4 == 0, named(packed, number // 4), named(ordinary, number - number // 4 - 1))
    mixed = jax.random.permutation(jax.random.fold_in(own, 3), amount)
    source_of, taker = mixed[0:amount // 2 * 2:2], mixed[1:amount // 2 * 2:2]
    room = jnp.minimum(tallies[source_of] - 1, bound - tallies[taker]) // 2
    room = jnp.where((source_of == order[0]) | (taker == order[0]) | (tallies[taker] == 0), 0, jnp.maximum(room, 0))
    passed = jax.random.randint(jax.random.fold_in(own, 4), (amount // 2,), 0, 1 << 20) % (room + 1)
    tallies = tallies.at[source_of].add(-passed).at[taker].add(passed)
    members = jnp.searchsorted(jnp.cumsum(tallies), jnp.arange(rows * top), side="right").astype(jnp.int32)
    table = members.reshape(top, rows).T
    table = table[jax.random.permutation(jax.random.fold_in(own, 1), rows)]
    offset_by = jax.random.randint(jax.random.fold_in(own, 2), (rows, 1), 0, top)
    return jnp.take_along_axis(table, (jnp.arange(top)[None, :] + offset_by) % top, axis=1)


def portions_of(number_of, total, most, lean, full):
    loads = [(1 << 20) // math.isqrt(standing ** lean) + 1 for standing in range(1, number_of + 1)]
    largest = most if full else min(most, max(-(-total // number_of), total * loads[0] // sum(loads)))
    least = 1 if total - largest >= number_of - 1 else 0
    holding, spare = [largest] + [least] * (number_of - 1), total - largest - least * (number_of - 1)
    while spare > 0:
        candidates = [i for i in range(1, number_of) if holding[i] < largest] or [i for i in range(1, number_of) if holding[i] < most]
        whole, left = sum([loads[i] for i in candidates]), spare
        for i in candidates:
            extra = min(most - holding[i], max(1, left * loads[i] // whole), spare)
            holding[i] = holding[i] + extra
            spare = spare - extra
    return np.array(holding)


def scatter_about(key, shape, scale, most, cuts=(), kind=jnp.bfloat16):
    entries = jax.random.normal(key, shape, jnp.float32) * scale
    if len(cuts) > 0:
        entries = level_of(key, shape, cuts, -0.22, 0.18) * entries
    return jnp.clip(entries, min=-most, max=most).astype(kind)


def setup_inputs(seed: int = 0) -> dict:
    key_of = jax.random.split(jax.random.key(seed), 13)
    residual_in = scatter_about(key_of[0], (ROWS, D), 1.0, 6.0, ((0, 512),))
    attention_out = scatter_about(key_of[1], (ROWS, HD), 1.0, 6.0, ((0, 512),))
    out_weight = scatter_about(key_of[2], (HD, D), HD ** -0.5, 0.125, ((1, 16),))
    post_gain = jnp.clip(1.0 + 0.18 * jax.random.normal(key_of[3], (D,), jnp.float32), 0.1, 1.9)
    router_weight = scatter_about(key_of[4], (D, EXPERTS), D ** -0.5, 0.125)
    expert_ids_keys = jax.random.split(jax.random.fold_in(key_of[5], 1), ROWS // ROW_DEV)
    expert_ids_turns = jax.random.permutation(jax.random.fold_in(key_of[5], 3), ROWS // ROW_DEV)
    expert_ids = jax.vmap(lambda own, number: deal_out(jax.random.fold_in(key_of[5], 2), own, number, ROW_DEV, EXPERTS, TOPK, CAP, 2))(expert_ids_keys, expert_ids_turns).reshape((ROWS, TOPK))
    expert_slot = jax.random.permutation(key_of[6], EXPERTS).astype(jnp.int32)
    expert_gate_up = scatter_about(key_of[7], (EXPERTS, D, 2 * F), D ** -0.5, 0.125, ((0, 32), (1, 16)))
    expert_down = scatter_about(key_of[8], (EXPERTS, F, D), F ** -0.5, 0.21875, ((0, 32), (2, 16)))
    shared_gate_up = scatter_about(key_of[9], (D, 2, FS), D ** -0.5, 0.125, ((2, 16),))
    shared_down = scatter_about(key_of[10], (FS, D), FS ** -0.5, 0.109375, ((1, 16),))
    final_gain = jnp.clip(1.0 + 0.18 * jax.random.normal(key_of[11], (D,), jnp.float32), 0.1, 1.9)
    return dict(residual_in=residual_in, attention_out=attention_out, out_weight=out_weight, post_gain=post_gain, router_weight=router_weight, expert_ids=expert_ids, expert_slot=expert_slot, expert_gate_up=expert_gate_up, expert_down=expert_down, shared_gate_up=shared_gate_up, shared_down=shared_down, final_gain=final_gain)


EPS = 1e-06

def rms_scale(values, gain):
    values = values.astype(jnp.float32)
    inverse = lax.rsqrt(lax.optimization_barrier(jnp.mean(values * values, axis=-1, keepdims=True)) + EPS)
    return values * inverse * gain

def reference(residual_in, attention_out, out_weight, post_gain, router_weight, expert_ids, expert_slot, expert_gate_up, expert_down, shared_gate_up, shared_down, final_gain):
    proj = jnp.dot(attention_out, out_weight, preferred_element_type=jnp.float32).astype(jnp.bfloat16)
    resid = (residual_in.astype(jnp.float32) + proj.astype(jnp.float32)).astype(jnp.bfloat16)
    normed = rms_scale(resid, post_gain).astype(jnp.bfloat16)
    logits = jnp.dot(normed, router_weight, preferred_element_type=jnp.float32)
    chosen = jnp.take_along_axis(logits, expert_ids, axis=1)
    raised = jnp.exp(chosen)
    gates = raised / lax.optimization_barrier(jnp.sum(raised, axis=1, keepdims=True))
    slots = expert_slot[expert_ids]
    assigned = ROW_DEV * TOPK
    flat_slots = slots.reshape(ROW_BLOCKS, assigned)
    marked = (flat_slots[:, :, None] == jnp.arange(EXPERTS, dtype=jnp.int32)[None, None, :]).astype(jnp.int32)
    before = jnp.cumsum(marked, axis=1) - marked
    position = lax.optimization_barrier(jnp.sum(before * marked, axis=2)).astype(jnp.int32)
    row_of = (jnp.arange(ROWS * TOPK, dtype=jnp.int32) // TOPK).reshape(ROW_BLOCKS, assigned)
    block_of = jnp.broadcast_to(jnp.arange(ROW_BLOCKS, dtype=jnp.int32)[:, None], (ROW_BLOCKS, assigned))
    row_table = jnp.zeros((EXPERTS, ROW_BLOCKS, CAP), jnp.int32).at[flat_slots, block_of, position].set(row_of)
    gate_table = jnp.zeros((EXPERTS, ROW_BLOCKS, CAP), jnp.float32).at[flat_slots, block_of, position].set(gates.reshape(ROW_BLOCKS, assigned))

    def serve(routed, slot):
        picked = row_table[slot].reshape(-1)
        inputs = normed[picked]
        both = jnp.dot(inputs, expert_gate_up[slot], preferred_element_type=jnp.float32)
        active = (jax.nn.silu(both[:, :F]) * both[:, F:]).astype(jnp.bfloat16)
        output = jnp.dot(active, expert_down[slot], preferred_element_type=jnp.float32).astype(jnp.bfloat16)
        weight = gate_table[slot].reshape(-1)
        return (routed.at[picked].add(weight[:, None] * output.astype(jnp.float32)), None)
    routed, _ = lax.scan(serve, jnp.zeros((ROWS, D), jnp.float32), jnp.arange(EXPERTS, dtype=jnp.int32))
    shared_both = jnp.dot(normed, shared_gate_up.reshape(D, 2 * FS), preferred_element_type=jnp.float32)
    shared_active = (jax.nn.silu(shared_both[:, :FS]) * shared_both[:, FS:]).astype(jnp.bfloat16)
    shared_out = jnp.dot(shared_active, shared_down, preferred_element_type=jnp.float32)
    total = resid.astype(jnp.float32) + routed + shared_out
    return rms_scale(total, final_gain).astype(jnp.bfloat16)
```

```python
import jax
import jax.numpy as jnp
from jax import lax
from jax.sharding import PartitionSpec as P

EPS = 1e-06


def gathered(array, axis):
    n = lax.axis_size(axis)
    me = lax.axis_index(axis)
    outs = [array] + [
        lax.ppermute(array, axis, [(s, (s + k) % n) for s in range(n)]) for k in range(1, n)
    ]
    stack = jnp.stack(outs)
    return jnp.take(stack, (me - jnp.arange(n)) % n, axis=0)


def in_order(blocks, dim):
    shape = list(blocks.shape[1:])
    shape[dim] *= blocks.shape[0]
    return jnp.moveaxis(blocks, 0, dim).reshape(shape)


def rms_scale(values, gain):
    values = values.astype(jnp.float32)
    inverse = lax.rsqrt(jnp.mean(values * values, axis=-1, keepdims=True) + EPS)
    return values * inverse * gain


def per_device(
    residual_in,
    attention_out,
    out_weight,
    post_gain,
    router_weight,
    expert_ids,
    expert_slot,
    expert_gate_up,
    expert_down,
    shared_gate_up,
    shared_down,
    final_gain,
):
    rows = residual_in.shape[0]
    width = residual_in.shape[1]
    experts = router_weight.shape[1]
    choose = expert_ids.shape[1]
    groups = lax.axis_size("dp")
    me = lax.axis_index("dp")
    capacity = max(2, min(rows, 2 * rows * choose // experts))

    both_in = jnp.concatenate([attention_out, residual_in], axis=1)
    group_in = gathered(both_in, "dp").reshape(groups * rows, 2 * width)
    group_attn = group_in[:, :width]
    group_resid_in = group_in[:, width:]
    proj_cols = jnp.dot(group_attn, out_weight, preferred_element_type=jnp.float32).astype(
        jnp.bfloat16
    )
    group_proj = in_order(gathered(proj_cols, "dp"), 1)
    group_resid = (group_resid_in.astype(jnp.float32) + group_proj.astype(jnp.float32)).astype(
        jnp.bfloat16
    )
    group_normed = rms_scale(group_resid, post_gain).astype(jnp.bfloat16)
    gate_up_part = expert_gate_up[0]
    down_turned = expert_down[0].T
    hidden_units = down_turned.shape[1]
    weights_part = jnp.concatenate([gate_up_part, down_turned], axis=1)
    weights_part, group_proj = lax.optimization_barrier((weights_part, group_proj))
    weights_full = in_order(gathered(weights_part, "dp"), 0)
    gate_up_full = weights_full[:, : 2 * hidden_units]
    down_turned_full = weights_full[:, 2 * hidden_units :]
    resid = lax.dynamic_slice_in_dim(group_resid, me * rows, rows, axis=0)
    normed = lax.dynamic_slice_in_dim(group_normed, me * rows, rows, axis=0)

    logits = jnp.dot(normed, router_weight, preferred_element_type=jnp.float32)
    expert_range = jnp.arange(experts, dtype=jnp.int32)
    picked = expert_ids[:, :, None] == expert_range[None, None, :]
    chosen = jnp.sum(jnp.where(picked, logits[:, None, :], 0.0), axis=2)
    raised = jnp.exp(chosen)
    gates = raised / jnp.sum(raised, axis=1, keepdims=True)
    slots = jnp.sum(jnp.where(picked, expert_slot[None, None, :], 0), axis=2).reshape(-1)
    marked = (slots[:, None] == expert_range[None, :]).astype(jnp.int32)
    before = jnp.cumsum(marked, axis=0) - marked
    position = jnp.sum(before * marked, axis=1)
    target = slots * capacity + position
    placed = target[:, None] == jnp.arange(experts * capacity, dtype=jnp.int32)[None, :]
    select = jnp.any(placed.reshape(rows, choose, experts * capacity), axis=1).astype(jnp.bfloat16)
    outgoing = jnp.einsum("rs,rd->sd", select, normed, preferred_element_type=jnp.float32)
    outgoing = outgoing.astype(jnp.bfloat16).reshape(experts, capacity, width)
    received = lax.all_to_all(outgoing, "expert", split_axis=0, concat_axis=0, tiled=True)
    sources, count, _ = received.shape
    flat = received.reshape(sources * count, width)
    both = jnp.dot(flat, gate_up_full, preferred_element_type=jnp.float32)
    active = (jax.nn.silu(both[:, :hidden_units]) * both[:, hidden_units:]).astype(jnp.bfloat16)
    result = lax.dot_general(
        active, down_turned_full, (((1,), (1,)), ((), ())), preferred_element_type=jnp.float32
    ).astype(jnp.bfloat16)
    result = result.reshape(sources, count, width)
    returned = lax.all_to_all(result, "expert", split_axis=0, concat_axis=0, tiled=True)

    shared_units = shared_gate_up.shape[2]
    shared_pair = shared_gate_up.reshape(width, 2 * shared_units)
    both = jnp.dot(group_normed, shared_pair, preferred_element_type=jnp.float32)
    shared_hidden = (jax.nn.silu(both[:, :shared_units]) * both[:, shared_units:]).astype(
        jnp.bfloat16
    )
    out_cols = jnp.dot(
        in_order(gathered(shared_hidden, "dp"), 1),
        shared_down,
        preferred_element_type=jnp.float32,
    )
    shared_out = lax.all_to_all(out_cols, "dp", split_axis=0, concat_axis=1, tiled=True)
    back_rows = jnp.take(returned.reshape(experts * capacity, width), target, axis=0)
    back_rows = back_rows.reshape(rows, choose, width).astype(jnp.float32)
    routed = jnp.sum(gates[:, :, None] * back_rows, axis=1)
    total = resid.astype(jnp.float32) + routed + shared_out
    return rms_scale(total, final_gain).astype(jnp.bfloat16)


def solution(mesh):
    in_specs = (
        P(("dp", "expert"), None),
        P(("dp", "expert"), None),
        P(None, "dp"),
        P(),
        P(),
        P(("dp", "expert"), None),
        P(),
        P("expert", "dp", None),
        P("expert", None, "dp"),
        P(None, None, "dp"),
        P(None, "dp"),
        P(),
    )
    out_specs = P(("dp", "expert"), None)
    return jax.shard_map(
        per_device, mesh=mesh, in_specs=in_specs, out_specs=out_specs, check_vma=False
    )
```

```python
import jax
import jax.numpy as jnp
from jax import lax
from jax.sharding import PartitionSpec as P

EPS = 1e-06


def in_order(blocks, dim):
    shape = list(blocks.shape[1:])
    shape[dim] *= blocks.shape[0]
    return jnp.moveaxis(blocks, 0, dim).reshape(shape)


def sent_to_all(array, axis):
    copies = jnp.broadcast_to(array, (lax.axis_size(axis), *array.shape))
    return lax.all_to_all(copies, axis, split_axis=0, concat_axis=0, tiled=True)


def collect(array, axis, dim):
    return in_order(sent_to_all(array, axis), dim)


def turned_gather(arrays, axis, dims):
    turned = [jnp.moveaxis(a, dim, 0) for a, dim in zip(arrays, dims)]
    widths = [t[0].size for t in turned]
    both = jnp.concatenate([t.reshape(-1, w) for t, w in zip(turned, widths)], axis=1)
    out = lax.all_gather(both, axis, axis=0, tiled=True)
    blocks = jnp.split(out, [sum(widths[:k]) for k in range(1, len(widths))], axis=1)
    return tuple(
        (
            jnp.moveaxis(b.reshape(-1, *t.shape[1:]), 0, dim)
            for b, t, dim in zip(blocks, turned, dims)
        )
    )


def rms_scale(values, gain):
    values = values.astype(jnp.float32)
    inverse = lax.rsqrt(jnp.mean(values * values, axis=-1, keepdims=True) + EPS)
    return values * inverse * gain


def per_device(
    residual_in,
    attention_out,
    out_weight,
    post_gain,
    router_weight,
    expert_ids,
    expert_slot,
    expert_gate_up,
    expert_down,
    shared_gate_up,
    shared_down,
    final_gain,
):
    rows = residual_in.shape[0]
    width = residual_in.shape[1]
    experts = router_weight.shape[1]
    choose = expert_ids.shape[1]
    capacity = max(2, min(rows, 2 * rows * choose // experts))
    proj_cols = jnp.dot(
        collect(attention_out, "dp", 0), out_weight, preferred_element_type=jnp.float32
    ).astype(jnp.bfloat16)
    proj = lax.all_to_all(proj_cols, "dp", split_axis=0, concat_axis=1, tiled=True)
    resid = (residual_in.astype(jnp.float32) + proj.astype(jnp.float32)).astype(jnp.bfloat16)
    normed = rms_scale(resid, post_gain).astype(jnp.bfloat16)
    logits = jnp.dot(normed, router_weight, preferred_element_type=jnp.float32)
    expert_range = jnp.arange(experts, dtype=jnp.int32)
    picked = expert_ids[:, :, None] == expert_range[None, None, :]
    chosen = jnp.sum(jnp.where(picked, logits[:, None, :], 0.0), axis=2)
    raised = jnp.exp(chosen)
    gates = raised / jnp.sum(raised, axis=1, keepdims=True)
    slots = jnp.sum(jnp.where(picked, expert_slot[None, None, :], 0), axis=2).reshape(-1)
    marked = (slots[:, None] == expert_range[None, :]).astype(jnp.int32)
    before = jnp.cumsum(marked, axis=0) - marked
    position = jnp.sum(before * marked, axis=1)
    target = slots * capacity + position
    placed = target[:, None] == jnp.arange(experts * capacity, dtype=jnp.int32)[None, :]
    select = jnp.any(placed.reshape(rows, choose, experts * capacity), axis=1).astype(jnp.bfloat16)
    outgoing = jnp.einsum("rs,rd->sd", select, normed, preferred_element_type=jnp.float32)
    outgoing = outgoing.astype(jnp.bfloat16).reshape(experts, capacity, width)
    gate_up_all, down_all = turned_gather((expert_gate_up, expert_down), "dp", (1, 2))
    gate_up_full = gate_up_all[0]
    down_full = down_all[0]
    hidden_units = gate_up_full.shape[1] // 2
    received = lax.all_to_all(outgoing, "expert", split_axis=0, concat_axis=0, tiled=True)
    sources, count, _ = received.shape
    flat = received.reshape(sources * count, width)
    both = jnp.dot(flat, gate_up_full, preferred_element_type=jnp.float32)
    active = (jax.nn.silu(both[:, :hidden_units]) * both[:, hidden_units:]).astype(jnp.bfloat16)
    result = jnp.dot(active, down_full, preferred_element_type=jnp.float32).astype(jnp.bfloat16)
    result = result.reshape(sources, count, width)
    returned = lax.all_to_all(result, "expert", split_axis=0, concat_axis=0, tiled=True)
    shared_units = shared_gate_up.shape[2]
    shared_pair = shared_gate_up.reshape(width, 2 * shared_units)
    normed_shared = normed + (gate_up_full[0, 0] * 0).astype(normed.dtype)
    both = jnp.dot(
        lax.all_gather(normed_shared, "dp", axis=0, tiled=True),
        shared_pair,
        preferred_element_type=jnp.float32,
    )
    shared_hidden = (jax.nn.silu(both[:, :shared_units]) * both[:, shared_units:]).astype(
        jnp.bfloat16
    )
    out_cols = jnp.dot(
        lax.all_gather(shared_hidden, "dp", axis=1, tiled=True),
        shared_down,
        preferred_element_type=jnp.float32,
    )
    shared_out = lax.all_to_all(out_cols, "dp", split_axis=0, concat_axis=1, tiled=True)
    back_rows = jnp.take(returned.reshape(experts * capacity, width), target, axis=0)
    back_rows = back_rows.reshape(rows, choose, width).astype(jnp.float32)
    routed = jnp.sum(gates[:, :, None] * back_rows, axis=1)
    total = resid.astype(jnp.float32) + routed + shared_out
    return rms_scale(total, final_gain).astype(jnp.bfloat16)


def solution(mesh):
    in_specs = (
        P(("dp", "expert"), None),
        P(("dp", "expert"), None),
        P(None, "dp"),
        P(),
        P(),
        P(("dp", "expert"), None),
        P(),
        P("expert", "dp", None),
        P("expert", None, "dp"),
        P(None, None, "dp"),
        P(None, "dp"),
        P(),
    )
    out_specs = P(("dp", "expert"), None)
    return jax.shard_map(
        per_device, mesh=mesh, in_specs=in_specs, out_specs=out_specs, check_vma=False
    )
```

```python
import jax
import jax.numpy as jnp
from jax import lax
from jax.sharding import PartitionSpec as P

EPS = 1e-06


def core_groups(axis):
    n = lax.axis_size(axis)
    return [list(range(0, n, 2)), list(range(1, n, 2))]


def with_sibling(blocks, axis):
    other = lax.ppermute(blocks, axis, [(i, i ^ 1) for i in range(lax.axis_size(axis))])
    pair = jnp.stack([blocks, other], axis=1)
    pair = jnp.where(lax.axis_index(axis) % 2 == 0, pair, jnp.flip(pair, axis=1))
    return pair.reshape(-1, *blocks.shape[1:])


def pair_gather(array, axis):
    blocks = lax.all_gather(array, axis, axis=0, axis_index_groups=core_groups(axis))
    return with_sibling(blocks, axis)


def pair_collect(array, axis):
    copies = jnp.broadcast_to(array, (lax.axis_size(axis) // 2, *array.shape))
    blocks = lax.all_to_all(
        copies, axis, 0, 0, tiled=True, axis_index_groups=core_groups(axis)
    )
    return with_sibling(blocks, axis)


def in_order(blocks, dim):
    shape = list(blocks.shape[1:])
    shape[dim] *= blocks.shape[0]
    return jnp.moveaxis(blocks, 0, dim).reshape(shape)


def sent_to_all(array, axis):
    copies = jnp.broadcast_to(array, (lax.axis_size(axis), *array.shape))
    return lax.all_to_all(copies, axis, split_axis=0, concat_axis=0, tiled=True)


def collect(array, axis, dim):
    return in_order(sent_to_all(array, axis), dim)


def turned_gather(arrays, axis, dims):
    turned = [jnp.moveaxis(a, dim, 0) for a, dim in zip(arrays, dims)]
    widths = [t[0].size for t in turned]
    both = jnp.concatenate([t.reshape(-1, w) for t, w in zip(turned, widths)], axis=1)
    out = lax.all_gather(both, axis, axis=0, tiled=True)
    blocks = jnp.split(out, [sum(widths[:k]) for k in range(1, len(widths))], axis=1)
    return tuple(
        (
            jnp.moveaxis(b.reshape(-1, *t.shape[1:]), 0, dim)
            for b, t, dim in zip(blocks, turned, dims)
        )
    )


def rms_scale(values, gain):
    values = values.astype(jnp.float32)
    inverse = lax.rsqrt(jnp.mean(values * values, axis=-1, keepdims=True) + EPS)
    return values * inverse * gain


def per_device(
    residual_in,
    attention_out,
    out_weight,
    post_gain,
    router_weight,
    expert_ids,
    expert_slot,
    expert_gate_up,
    expert_down,
    shared_gate_up,
    shared_down,
    final_gain,
):
    rows = residual_in.shape[0]
    width = residual_in.shape[1]
    experts = router_weight.shape[1]
    choose = expert_ids.shape[1]
    capacity = max(2, min(rows, 2 * rows * choose // experts))
    group_attn = in_order(pair_collect(attention_out, "dp"), 0)
    proj_cols = jnp.dot(group_attn, out_weight, preferred_element_type=jnp.float32).astype(
        jnp.bfloat16
    )
    proj = lax.all_to_all(proj_cols, "dp", split_axis=0, concat_axis=1, tiled=True)
    resid = (residual_in.astype(jnp.float32) + proj.astype(jnp.float32)).astype(jnp.bfloat16)
    normed = rms_scale(resid, post_gain).astype(jnp.bfloat16)
    logits = jnp.dot(normed, router_weight, preferred_element_type=jnp.float32)
    expert_range = jnp.arange(experts, dtype=jnp.int32)
    picked = expert_ids[:, :, None] == expert_range[None, None, :]
    chosen = jnp.sum(jnp.where(picked, logits[:, None, :], 0.0), axis=2)
    raised = jnp.exp(chosen)
    gates = raised / jnp.sum(raised, axis=1, keepdims=True)
    slots = jnp.sum(jnp.where(picked, expert_slot[None, None, :], 0), axis=2).reshape(-1)
    marked = (slots[:, None] == expert_range[None, :]).astype(jnp.int32)
    before = jnp.cumsum(marked, axis=0) - marked
    position = jnp.sum(before * marked, axis=1)
    target = slots * capacity + position
    placed = target[:, None] == jnp.arange(experts * capacity, dtype=jnp.int32)[None, :]
    select = jnp.any(placed.reshape(rows, choose, experts * capacity), axis=1).astype(jnp.bfloat16)
    outgoing = jnp.einsum("rs,rd->sd", select, normed, preferred_element_type=jnp.float32)
    outgoing = outgoing.astype(jnp.bfloat16).reshape(experts, capacity, width)
    hidden_units = expert_down.shape[1]
    weights_part = jnp.concatenate([expert_gate_up[0], expert_down[0].T], axis=1)
    weights_blocks = lax.all_gather(
        weights_part, "dp", axis=0, axis_index_groups=core_groups("dp")
    )
    received = lax.all_to_all(outgoing, "expert", split_axis=0, concat_axis=0, tiled=True)
    weights_blocks = weights_blocks + (received[0, 0, 0] * 0).astype(weights_blocks.dtype)
    weights_full = in_order(with_sibling(weights_blocks, "dp"), 0)
    gate_up_full = weights_full[:, : 2 * hidden_units]
    down_turned_full = weights_full[:, 2 * hidden_units :]
    sources, count, _ = received.shape
    flat = received.reshape(sources * count, width)
    both = jnp.dot(flat, gate_up_full, preferred_element_type=jnp.float32)
    active = (jax.nn.silu(both[:, :hidden_units]) * both[:, hidden_units:]).astype(jnp.bfloat16)
    result = lax.dot_general(
        active, down_turned_full, (((1,), (1,)), ((), ())), preferred_element_type=jnp.float32
    ).astype(jnp.bfloat16)
    result = result.reshape(sources, count, width)
    returned = lax.all_to_all(result, "expert", split_axis=0, concat_axis=0, tiled=True)
    shared_units = shared_gate_up.shape[2]
    shared_pair = shared_gate_up.reshape(width, 2 * shared_units)
    normed_shared = normed
    both = jnp.dot(
        in_order(pair_gather(normed_shared, "dp"), 0),
        shared_pair,
        preferred_element_type=jnp.float32,
    )
    shared_hidden = (jax.nn.silu(both[:, :shared_units]) * both[:, shared_units:]).astype(
        jnp.bfloat16
    )
    out_cols = jnp.dot(
        in_order(pair_gather(shared_hidden, "dp"), 1),
        shared_down,
        preferred_element_type=jnp.float32,
    )
    shared_out = lax.all_to_all(out_cols, "dp", split_axis=0, concat_axis=1, tiled=True)
    back_rows = jnp.take(returned.reshape(experts * capacity, width), target, axis=0)
    back_rows = back_rows.reshape(rows, choose, width).astype(jnp.float32)
    routed = jnp.sum(gates[:, :, None] * back_rows, axis=1)
    total = resid.astype(jnp.float32) + routed + shared_out
    return rms_scale(total, final_gain).astype(jnp.bfloat16)


def solution(mesh):
    in_specs = (
        P(("dp", "expert"), None),
        P(("dp", "expert"), None),
        P(None, "dp"),
        P(),
        P(),
        P(("dp", "expert"), None),
        P(),
        P("expert", "dp", None),
        P("expert", None, "dp"),
        P(None, None, "dp"),
        P(None, "dp"),
        P(),
    )
    out_specs = P(("dp", "expert"), None)
    return jax.shard_map(
        per_device, mesh=mesh, in_specs=in_specs, out_specs=out_specs, check_vma=False
    )
```

```python
import jax
import jax.numpy as jnp
from jax import lax
from jax.sharding import PartitionSpec as P

EPS = 1e-06


def core_groups(axis):
    n = lax.axis_size(axis)
    return [list(range(0, n, 2)), list(range(1, n, 2))]


def with_sibling(blocks, axis):
    other = lax.ppermute(blocks, axis, [(i, i ^ 1) for i in range(lax.axis_size(axis))])
    pair = jnp.stack([blocks, other], axis=1)
    pair = jnp.where(lax.axis_index(axis) % 2 == 0, pair, jnp.flip(pair, axis=1))
    return pair.reshape(-1, *blocks.shape[1:])


def pair_collect(array, axis):
    copies = jnp.broadcast_to(array, (lax.axis_size(axis) // 2, *array.shape))
    blocks = lax.all_to_all(
        copies, axis, 0, 0, tiled=True, axis_index_groups=core_groups(axis)
    )
    return with_sibling(blocks, axis)


def in_order(blocks, dim):
    shape = list(blocks.shape[1:])
    shape[dim] *= blocks.shape[0]
    return jnp.moveaxis(blocks, 0, dim).reshape(shape)


def sent_to_all(array, axis):
    copies = jnp.broadcast_to(array, (lax.axis_size(axis), *array.shape))
    return lax.all_to_all(copies, axis, split_axis=0, concat_axis=0, tiled=True)


def collect(array, axis, dim):
    return in_order(sent_to_all(array, axis), dim)


def turned_gather(arrays, axis, dims):
    turned = [jnp.moveaxis(a, dim, 0) for a, dim in zip(arrays, dims)]
    widths = [t[0].size for t in turned]
    both = jnp.concatenate([t.reshape(-1, w) for t, w in zip(turned, widths)], axis=1)
    out = lax.all_gather(both, axis, axis=0, tiled=True)
    blocks = jnp.split(out, [sum(widths[:k]) for k in range(1, len(widths))], axis=1)
    return tuple(
        (
            jnp.moveaxis(b.reshape(-1, *t.shape[1:]), 0, dim)
            for b, t, dim in zip(blocks, turned, dims)
        )
    )


def rms_scale(values, gain):
    values = values.astype(jnp.float32)
    inverse = lax.rsqrt(jnp.mean(values * values, axis=-1, keepdims=True) + EPS)
    return values * inverse * gain


def per_device(
    residual_in,
    attention_out,
    out_weight,
    post_gain,
    router_weight,
    expert_ids,
    expert_slot,
    expert_gate_up,
    expert_down,
    shared_gate_up,
    shared_down,
    final_gain,
):
    rows = residual_in.shape[0]
    width = residual_in.shape[1]
    experts = router_weight.shape[1]
    choose = expert_ids.shape[1]
    capacity = max(2, min(rows, 2 * rows * choose // experts))
    proj_cols = jnp.dot(
        in_order(pair_collect(attention_out, "dp"), 0), out_weight, preferred_element_type=jnp.float32
    ).astype(jnp.bfloat16)
    proj = lax.all_to_all(proj_cols, "dp", split_axis=0, concat_axis=1, tiled=True)
    resid = (residual_in.astype(jnp.float32) + proj.astype(jnp.float32)).astype(jnp.bfloat16)
    normed = rms_scale(resid, post_gain).astype(jnp.bfloat16)
    logits = jnp.dot(normed, router_weight, preferred_element_type=jnp.float32)
    expert_range = jnp.arange(experts, dtype=jnp.int32)
    picked = expert_ids[:, :, None] == expert_range[None, None, :]
    chosen = jnp.sum(jnp.where(picked, logits[:, None, :], 0.0), axis=2)
    raised = jnp.exp(chosen)
    gates = raised / jnp.sum(raised, axis=1, keepdims=True)
    slots = jnp.sum(jnp.where(picked, expert_slot[None, None, :], 0), axis=2).reshape(-1)
    marked = (slots[:, None] == expert_range[None, :]).astype(jnp.int32)
    before = jnp.cumsum(marked, axis=0) - marked
    position = jnp.sum(before * marked, axis=1)
    target = slots * capacity + position
    placed = target[:, None] == jnp.arange(experts * capacity, dtype=jnp.int32)[None, :]
    select = jnp.any(placed.reshape(rows, choose, experts * capacity), axis=1).astype(jnp.bfloat16)
    outgoing = jnp.einsum("rs,rd->sd", select, normed, preferred_element_type=jnp.float32)
    outgoing = outgoing.astype(jnp.bfloat16).reshape(experts, capacity, width)
    gate_up_all, down_all = turned_gather((expert_gate_up, expert_down), "dp", (1, 2))
    gate_up_full = gate_up_all[0]
    down_full = down_all[0]
    hidden_units = gate_up_full.shape[1] // 2
    received = lax.all_to_all(outgoing, "expert", split_axis=0, concat_axis=0, tiled=True)
    sources, count, _ = received.shape
    flat = received.reshape(sources * count, width)
    both = jnp.dot(flat, gate_up_full, preferred_element_type=jnp.float32)
    active = (jax.nn.silu(both[:, :hidden_units]) * both[:, hidden_units:]).astype(jnp.bfloat16)
    result = jnp.dot(active, down_full, preferred_element_type=jnp.float32).astype(jnp.bfloat16)
    result = result.reshape(sources, count, width)
    returned = lax.all_to_all(result, "expert", split_axis=0, concat_axis=0, tiled=True)
    shared_units = shared_gate_up.shape[2]
    shared_pair = shared_gate_up.reshape(width, 2 * shared_units)
    both = jnp.dot(
        lax.all_gather(normed, "dp", axis=0, tiled=True),
        shared_pair,
        preferred_element_type=jnp.float32,
    )
    shared_hidden = (jax.nn.silu(both[:, :shared_units]) * both[:, shared_units:]).astype(
        jnp.bfloat16
    )
    out_cols = jnp.dot(
        lax.all_gather(shared_hidden, "dp", axis=1, tiled=True),
        shared_down,
        preferred_element_type=jnp.float32,
    )
    shared_out = lax.all_to_all(out_cols, "dp", split_axis=0, concat_axis=1, tiled=True)
    back_rows = jnp.take(returned.reshape(experts * capacity, width), target, axis=0)
    back_rows = back_rows.reshape(rows, choose, width).astype(jnp.float32)
    routed = jnp.sum(gates[:, :, None] * back_rows, axis=1)
    total = resid.astype(jnp.float32) + routed + shared_out
    return rms_scale(total, final_gain).astype(jnp.bfloat16)


def solution(mesh):
    in_specs = (
        P(("dp", "expert"), None),
        P(("dp", "expert"), None),
        P(None, "dp"),
        P(),
        P(),
        P(("dp", "expert"), None),
        P(),
        P("expert", "dp", None),
        P("expert", None, "dp"),
        P(None, None, "dp"),
        P(None, "dp"),
        P(),
    )
    out_specs = P(("dp", "expert"), None)
    return jax.shard_map(
        per_device, mesh=mesh, in_specs=in_specs, out_specs=out_specs, check_vma=False
    )
```

```python
import jax
import jax.numpy as jnp
from jax import lax
from jax.sharding import PartitionSpec as P

EPS = 1e-06


def core_groups(axis):
    n = lax.axis_size(axis)
    return [list(range(0, n, 2)), list(range(1, n, 2))]


def with_sibling(blocks, axis):
    other = lax.ppermute(blocks, axis, [(i, i ^ 1) for i in range(lax.axis_size(axis))])
    pair = jnp.stack([blocks, other], axis=1)
    pair = jnp.where(lax.axis_index(axis) % 2 == 0, pair, jnp.flip(pair, axis=1))
    return pair.reshape(-1, *blocks.shape[1:])


def pair_collect(array, axis):
    copies = jnp.broadcast_to(array, (lax.axis_size(axis) // 2, *array.shape))
    blocks = lax.all_to_all(
        copies, axis, 0, 0, tiled=True, axis_index_groups=core_groups(axis)
    )
    return with_sibling(blocks, axis)


def in_order(blocks, dim):
    shape = list(blocks.shape[1:])
    shape[dim] *= blocks.shape[0]
    return jnp.moveaxis(blocks, 0, dim).reshape(shape)


def sent_to_all(array, axis):
    copies = jnp.broadcast_to(array, (lax.axis_size(axis), *array.shape))
    return lax.all_to_all(copies, axis, split_axis=0, concat_axis=0, tiled=True)


def collect(array, axis, dim):
    return in_order(sent_to_all(array, axis), dim)


def turned_gather(arrays, axis, dims):
    turned = [jnp.moveaxis(a, dim, 0) for a, dim in zip(arrays, dims)]
    widths = [t[0].size for t in turned]
    both = jnp.concatenate([t.reshape(-1, w) for t, w in zip(turned, widths)], axis=1)
    out = lax.all_gather(both, axis, axis=0, tiled=True)
    blocks = jnp.split(out, [sum(widths[:k]) for k in range(1, len(widths))], axis=1)
    return tuple(
        (
            jnp.moveaxis(b.reshape(-1, *t.shape[1:]), 0, dim)
            for b, t, dim in zip(blocks, turned, dims)
        )
    )


def rms_scale(values, gain):
    values = values.astype(jnp.float32)
    inverse = lax.rsqrt(jnp.mean(values * values, axis=-1, keepdims=True) + EPS)
    return values * inverse * gain


def per_device(
    residual_in,
    attention_out,
    out_weight,
    post_gain,
    router_weight,
    expert_ids,
    expert_slot,
    expert_gate_up,
    expert_down,
    shared_gate_up,
    shared_down,
    final_gain,
):
    rows = residual_in.shape[0]
    width = residual_in.shape[1]
    experts = router_weight.shape[1]
    choose = expert_ids.shape[1]
    capacity = max(2, min(rows, 2 * rows * choose // experts))
    proj_cols = jnp.dot(
        in_order(pair_collect(attention_out, "dp"), 0), out_weight, preferred_element_type=jnp.float32
    ).astype(jnp.bfloat16)
    proj = lax.all_to_all(proj_cols, "dp", split_axis=0, concat_axis=1, tiled=True)
    resid = (residual_in.astype(jnp.float32) + proj.astype(jnp.float32)).astype(jnp.bfloat16)
    normed = rms_scale(resid, post_gain).astype(jnp.bfloat16)
    logits = jnp.dot(normed, router_weight, preferred_element_type=jnp.float32)
    expert_range = jnp.arange(experts, dtype=jnp.int32)
    picked = expert_ids[:, :, None] == expert_range[None, None, :]
    chosen = jnp.sum(jnp.where(picked, logits[:, None, :], 0.0), axis=2)
    raised = jnp.exp(chosen)
    gates = raised / jnp.sum(raised, axis=1, keepdims=True)
    slots = jnp.sum(jnp.where(picked, expert_slot[None, None, :], 0), axis=2).reshape(-1)
    marked = (slots[:, None] == expert_range[None, :]).astype(jnp.int32)
    before = jnp.cumsum(marked, axis=0) - marked
    position = jnp.sum(before * marked, axis=1)
    target = slots * capacity + position
    placed = target[:, None] == jnp.arange(experts * capacity, dtype=jnp.int32)[None, :]
    select = jnp.any(placed.reshape(rows, choose, experts * capacity), axis=1).astype(jnp.bfloat16)
    outgoing = jnp.einsum("rs,rd->sd", select, normed, preferred_element_type=jnp.float32)
    outgoing = outgoing.astype(jnp.bfloat16).reshape(experts, capacity, width)
    gate_up_all, down_all = turned_gather((expert_gate_up, expert_down), "dp", (1, 2))
    gate_up_full = gate_up_all[0]
    down_full = down_all[0]
    hidden_units = gate_up_full.shape[1] // 2
    received = lax.all_to_all(outgoing, "expert", split_axis=0, concat_axis=0, tiled=True)
    sources, count, _ = received.shape
    flat = received.reshape(sources * count, width)
    both = jnp.dot(flat, gate_up_full, preferred_element_type=jnp.float32)
    active = (jax.nn.silu(both[:, :hidden_units]) * both[:, hidden_units:]).astype(jnp.bfloat16)
    result = jnp.dot(active, down_full, preferred_element_type=jnp.float32).astype(jnp.bfloat16)
    result = result.reshape(sources, count, width)
    returned = lax.all_to_all(result, "expert", split_axis=0, concat_axis=0, tiled=True)
    shared_units = shared_gate_up.shape[2]
    shared_pair = shared_gate_up.reshape(width, 2 * shared_units)
    normed_shared = normed + (gate_up_full[0, 0] * 0 + outgoing[0, 0, 0] * 0).astype(normed.dtype)
    both = jnp.dot(
        lax.all_gather(normed_shared, "dp", axis=0, tiled=True),
        shared_pair,
        preferred_element_type=jnp.float32,
    )
    shared_hidden = (jax.nn.silu(both[:, :shared_units]) * both[:, shared_units:]).astype(
        jnp.bfloat16
    )
    out_cols = jnp.dot(
        lax.all_gather(shared_hidden, "dp", axis=1, tiled=True),
        shared_down,
        preferred_element_type=jnp.float32,
    )
    shared_out = lax.all_to_all(out_cols, "dp", split_axis=0, concat_axis=1, tiled=True)
    back_rows = jnp.take(returned.reshape(experts * capacity, width), target, axis=0)
    back_rows = back_rows.reshape(rows, choose, width).astype(jnp.float32)
    routed = jnp.sum(gates[:, :, None] * back_rows, axis=1)
    total = resid.astype(jnp.float32) + routed + shared_out
    return rms_scale(total, final_gain).astype(jnp.bfloat16)


def solution(mesh):
    in_specs = (
        P(("dp", "expert"), None),
        P(("dp", "expert"), None),
        P(None, "dp"),
        P(),
        P(),
        P(("dp", "expert"), None),
        P(),
        P("expert", "dp", None),
        P("expert", None, "dp"),
        P(None, None, "dp"),
        P(None, "dp"),
        P(),
    )
    out_specs = P(("dp", "expert"), None)
    return jax.shard_map(
        per_device, mesh=mesh, in_specs=in_specs, out_specs=out_specs, check_vma=False
    )
```

```python
import jax
import jax.numpy as jnp
from jax import lax
from jax.sharding import PartitionSpec as P

EPS = 1e-06


def core_groups(axis):
    n = lax.axis_size(axis)
    return [list(range(0, n, 2)), list(range(1, n, 2))]


def with_sibling(blocks, axis):
    other = lax.ppermute(blocks, axis, [(i, i ^ 1) for i in range(lax.axis_size(axis))])
    pair = jnp.stack([blocks, other], axis=1)
    pair = jnp.where(lax.axis_index(axis) % 2 == 0, pair, jnp.flip(pair, axis=1))
    return pair.reshape(-1, *blocks.shape[1:])


def pair_collect(array, axis):
    copies = jnp.broadcast_to(array, (lax.axis_size(axis) // 2, *array.shape))
    blocks = lax.all_to_all(
        copies, axis, 0, 0, tiled=True, axis_index_groups=core_groups(axis)
    )
    return with_sibling(blocks, axis)


def in_order(blocks, dim):
    shape = list(blocks.shape[1:])
    shape[dim] *= blocks.shape[0]
    return jnp.moveaxis(blocks, 0, dim).reshape(shape)


def sent_to_all(array, axis):
    copies = jnp.broadcast_to(array, (lax.axis_size(axis), *array.shape))
    return lax.all_to_all(copies, axis, split_axis=0, concat_axis=0, tiled=True)


def collect(array, axis, dim):
    return in_order(sent_to_all(array, axis), dim)


def turned_gather(arrays, axis, dims):
    turned = [jnp.moveaxis(a, dim, 0) for a, dim in zip(arrays, dims)]
    widths = [t[0].size for t in turned]
    both = jnp.concatenate([t.reshape(-1, w) for t, w in zip(turned, widths)], axis=1)
    out = lax.all_gather(both, axis, axis=0, tiled=True)
    blocks = jnp.split(out, [sum(widths[:k]) for k in range(1, len(widths))], axis=1)
    return tuple(
        (
            jnp.moveaxis(b.reshape(-1, *t.shape[1:]), 0, dim)
            for b, t, dim in zip(blocks, turned, dims)
        )
    )


def rms_scale(values, gain):
    values = values.astype(jnp.float32)
    inverse = lax.rsqrt(jnp.mean(values * values, axis=-1, keepdims=True) + EPS)
    return values * inverse * gain


def per_device(
    residual_in,
    attention_out,
    out_weight,
    post_gain,
    router_weight,
    expert_ids,
    expert_slot,
    expert_gate_up,
    expert_down,
    shared_gate_up,
    shared_down,
    final_gain,
):
    rows = residual_in.shape[0]
    width = residual_in.shape[1]
    experts = router_weight.shape[1]
    choose = expert_ids.shape[1]
    capacity = max(2, min(rows, 2 * rows * choose // experts))
    proj_cols = jnp.dot(
        in_order(pair_collect(attention_out, "dp"), 0), out_weight, preferred_element_type=jnp.float32
    ).astype(jnp.bfloat16)
    proj = lax.all_to_all(proj_cols, "dp", split_axis=0, concat_axis=1, tiled=True)
    resid = (residual_in.astype(jnp.float32) + proj.astype(jnp.float32)).astype(jnp.bfloat16)
    normed = rms_scale(resid, post_gain).astype(jnp.bfloat16)
    logits = jnp.dot(normed, router_weight, preferred_element_type=jnp.float32)
    expert_range = jnp.arange(experts, dtype=jnp.int32)
    picked = expert_ids[:, :, None] == expert_range[None, None, :]
    chosen = jnp.sum(jnp.where(picked, logits[:, None, :], 0.0), axis=2)
    raised = jnp.exp(chosen)
    gates = raised / jnp.sum(raised, axis=1, keepdims=True)
    slots = jnp.sum(jnp.where(picked, expert_slot[None, None, :], 0), axis=2).reshape(-1)
    marked = (slots[:, None] == expert_range[None, :]).astype(jnp.int32)
    before = jnp.cumsum(marked, axis=0) - marked
    position = jnp.sum(before * marked, axis=1)
    target = slots * capacity + position
    placed = target[:, None] == jnp.arange(experts * capacity, dtype=jnp.int32)[None, :]
    select = jnp.any(placed.reshape(rows, choose, experts * capacity), axis=1).astype(jnp.bfloat16)
    outgoing = jnp.einsum("rs,rd->sd", select, normed, preferred_element_type=jnp.float32)
    outgoing = outgoing.astype(jnp.bfloat16).reshape(experts, capacity, width)
    gate_up_all, down_all = turned_gather((expert_gate_up, expert_down), "dp", (1, 2))
    gate_up_full = gate_up_all[0]
    down_full = down_all[0]
    hidden_units = gate_up_full.shape[1] // 2
    received = lax.all_to_all(outgoing, "expert", split_axis=0, concat_axis=0, tiled=True)
    sources, count, _ = received.shape
    flat = received.reshape(sources * count, width)
    both = jnp.dot(flat, gate_up_full, preferred_element_type=jnp.float32)
    active = (jax.nn.silu(both[:, :hidden_units]) * both[:, hidden_units:]).astype(jnp.bfloat16)
    result = jnp.dot(active, down_full, preferred_element_type=jnp.float32).astype(jnp.bfloat16)
    result = result.reshape(sources, count, width)
    returned = lax.all_to_all(result, "expert", split_axis=0, concat_axis=0, tiled=True)
    shared_units = shared_gate_up.shape[2]
    shared_pair = shared_gate_up.reshape(width, 2 * shared_units)
    normed_shared = normed + (gate_up_full[0, 0] * 0 + outgoing[0, 0, 0] * 0).astype(normed.dtype)
    both = jnp.dot(
        lax.all_gather(normed_shared, "dp", axis=0, tiled=True),
        shared_pair,
        preferred_element_type=jnp.float32,
    )
    shared_hidden = (jax.nn.silu(both[:, :shared_units]) * both[:, shared_units:]).astype(
        jnp.bfloat16
    )
    out_cols = jnp.dot(
        lax.all_gather(shared_hidden, "dp", axis=1, tiled=True),
        shared_down,
        preferred_element_type=jnp.float32,
    )
    shared_out = lax.all_to_all(out_cols, "dp", split_axis=0, concat_axis=1, tiled=True)
    weighted = jnp.sum(
        placed.reshape(rows, choose, experts * capacity) * gates[:, :, None], axis=1
    )
    routed = jnp.dot(
        weighted,
        returned.reshape(experts * capacity, width).astype(jnp.float32),
        precision=lax.Precision.HIGHEST,
        preferred_element_type=jnp.float32,
    )
    total = resid.astype(jnp.float32) + routed + shared_out
    return rms_scale(total, final_gain).astype(jnp.bfloat16)


def solution(mesh):
    in_specs = (
        P(("dp", "expert"), None),
        P(("dp", "expert"), None),
        P(None, "dp"),
        P(),
        P(),
        P(("dp", "expert"), None),
        P(),
        P("expert", "dp", None),
        P("expert", None, "dp"),
        P(None, None, "dp"),
        P(None, "dp"),
        P(),
    )
    out_specs = P(("dp", "expert"), None)
    return jax.shard_map(
        per_device, mesh=mesh, in_specs=in_specs, out_specs=out_specs, check_vma=False
    )
```

```python
import jax
import jax.numpy as jnp
from jax import lax
from jax.sharding import PartitionSpec as P

EPS = 1e-06


def core_groups(axis):
    n = lax.axis_size(axis)
    return [list(range(0, n, 2)), list(range(1, n, 2))]


def with_sibling(blocks, axis):
    other = lax.ppermute(blocks, axis, [(i, i ^ 1) for i in range(lax.axis_size(axis))])
    pair = jnp.stack([blocks, other], axis=1)
    pair = jnp.where(lax.axis_index(axis) % 2 == 0, pair, jnp.flip(pair, axis=1))
    return pair.reshape(-1, *blocks.shape[1:])


def pair_collect(array, axis):
    copies = jnp.broadcast_to(array, (lax.axis_size(axis) // 2, *array.shape))
    blocks = lax.all_to_all(
        copies, axis, 0, 0, tiled=True, axis_index_groups=core_groups(axis)
    )
    return with_sibling(blocks, axis)


def in_order(blocks, dim):
    shape = list(blocks.shape[1:])
    shape[dim] *= blocks.shape[0]
    return jnp.moveaxis(blocks, 0, dim).reshape(shape)


def sent_to_all(array, axis):
    copies = jnp.broadcast_to(array, (lax.axis_size(axis), *array.shape))
    return lax.all_to_all(copies, axis, split_axis=0, concat_axis=0, tiled=True)


def collect(array, axis, dim):
    return in_order(sent_to_all(array, axis), dim)


def turned_gather(arrays, axis, dims):
    turned = [jnp.moveaxis(a, dim, 0) for a, dim in zip(arrays, dims)]
    widths = [t[0].size for t in turned]
    both = jnp.concatenate([t.reshape(-1, w) for t, w in zip(turned, widths)], axis=1)
    out = lax.all_gather(both, axis, axis=0, tiled=True)
    blocks = jnp.split(out, [sum(widths[:k]) for k in range(1, len(widths))], axis=1)
    return tuple(
        (
            jnp.moveaxis(b.reshape(-1, *t.shape[1:]), 0, dim)
            for b, t, dim in zip(blocks, turned, dims)
        )
    )


def rms_scale(values, gain):
    values = values.astype(jnp.float32)
    inverse = lax.rsqrt(jnp.mean(values * values, axis=-1, keepdims=True) + EPS)
    return values * inverse * gain


def per_device(
    residual_in,
    attention_out,
    out_weight,
    post_gain,
    router_weight,
    expert_ids,
    expert_slot,
    expert_gate_up,
    expert_down,
    shared_gate_up,
    shared_down,
    final_gain,
):
    rows = residual_in.shape[0]
    width = residual_in.shape[1]
    experts = router_weight.shape[1]
    choose = expert_ids.shape[1]
    capacity = max(2, min(rows, 2 * rows * choose // experts))
    proj_cols = jnp.dot(
        in_order(pair_collect(attention_out, "dp"), 0), out_weight, preferred_element_type=jnp.float32
    ).astype(jnp.bfloat16)
    proj = lax.all_to_all(proj_cols, "dp", split_axis=0, concat_axis=1, tiled=True)
    resid = (residual_in.astype(jnp.float32) + proj.astype(jnp.float32)).astype(jnp.bfloat16)
    normed = rms_scale(resid, post_gain).astype(jnp.bfloat16)
    logits = jnp.dot(normed, router_weight, preferred_element_type=jnp.float32)
    expert_range = jnp.arange(experts, dtype=jnp.int32)
    picked = expert_ids[:, :, None] == expert_range[None, None, :]
    chosen = jnp.sum(jnp.where(picked, logits[:, None, :], 0.0), axis=2)
    raised = jnp.exp(chosen)
    gates = raised / jnp.sum(raised, axis=1, keepdims=True)
    slots = jnp.sum(jnp.where(picked, expert_slot[None, None, :], 0), axis=2).reshape(-1)
    marked = (slots[:, None] == expert_range[None, :]).astype(jnp.int32)
    before = jnp.cumsum(marked, axis=0) - marked
    position = jnp.sum(before * marked, axis=1)
    target = slots * capacity + position
    placed = target[:, None] == jnp.arange(experts * capacity, dtype=jnp.int32)[None, :]
    select = jnp.any(placed.reshape(rows, choose, experts * capacity), axis=1).astype(jnp.bfloat16)
    outgoing = jnp.einsum("rs,rd->sd", select, normed, preferred_element_type=jnp.float32)
    outgoing = outgoing.astype(jnp.bfloat16).reshape(experts, capacity, width)
    gate_up_all, down_all = turned_gather((expert_gate_up, expert_down), "dp", (1, 2))
    gate_up_full = gate_up_all[0]
    down_full = down_all[0]
    hidden_units = gate_up_full.shape[1] // 2
    received = lax.all_to_all(outgoing, "expert", split_axis=0, concat_axis=0, tiled=True)
    sources, count, _ = received.shape
    flat = received.reshape(sources * count, width)
    both = jnp.dot(flat, gate_up_full, preferred_element_type=jnp.float32)
    active = (jax.nn.silu(both[:, :hidden_units]) * both[:, hidden_units:]).astype(jnp.bfloat16)
    result = jnp.dot(active, down_full, preferred_element_type=jnp.float32).astype(jnp.bfloat16)
    result = result.reshape(sources, count, width)
    returned = lax.all_to_all(result, "expert", split_axis=0, concat_axis=0, tiled=True)
    shared_units = shared_gate_up.shape[2]
    shared_pair = shared_gate_up.reshape(width, 2 * shared_units)
    normed_shared = normed + (gate_up_full[0, 0] * 0 + outgoing[0, 0, 0] * 0).astype(normed.dtype)
    both = jnp.dot(
        lax.all_gather(normed_shared, "dp", axis=0, tiled=True),
        shared_pair,
        preferred_element_type=jnp.float32,
    )
    shared_hidden = (jax.nn.silu(both[:, :shared_units]) * both[:, shared_units:]).astype(
        jnp.bfloat16
    )
    out_cols = jnp.dot(
        lax.all_gather(shared_hidden, "dp", axis=1, tiled=True),
        shared_down,
        preferred_element_type=jnp.float32,
    )
    shared_out = lax.all_to_all(
        out_cols.astype(jnp.bfloat16), "dp", split_axis=0, concat_axis=1, tiled=True
    ).astype(jnp.float32)
    weighted = jnp.sum(
        placed.reshape(rows, choose, experts * capacity) * gates[:, :, None], axis=1
    )
    routed = jnp.dot(
        weighted,
        returned.reshape(experts * capacity, width).astype(jnp.float32),
        precision=lax.Precision.HIGHEST,
        preferred_element_type=jnp.float32,
    )
    total = resid.astype(jnp.float32) + routed + shared_out
    return rms_scale(total, final_gain).astype(jnp.bfloat16)


def solution(mesh):
    in_specs = (
        P(("dp", "expert"), None),
        P(("dp", "expert"), None),
        P(None, "dp"),
        P(),
        P(),
        P(("dp", "expert"), None),
        P(),
        P("expert", "dp", None),
        P("expert", None, "dp"),
        P(None, None, "dp"),
        P(None, "dp"),
        P(),
    )
    out_specs = P(("dp", "expert"), None)
    return jax.shard_map(
        per_device, mesh=mesh, in_specs=in_specs, out_specs=out_specs, check_vma=False
    )
```

```python
import jax
import jax.numpy as jnp
from jax import lax
from jax.sharding import PartitionSpec as P

EPS = 1e-06


def core_groups(axis):
    n = lax.axis_size(axis)
    return [list(range(0, n, 2)), list(range(1, n, 2))]


def with_sibling(blocks, axis):
    other = lax.ppermute(blocks, axis, [(i, i ^ 1) for i in range(lax.axis_size(axis))])
    pair = jnp.stack([blocks, other], axis=1)
    pair = jnp.where(lax.axis_index(axis) % 2 == 0, pair, jnp.flip(pair, axis=1))
    return pair.reshape(-1, *blocks.shape[1:])


def pair_collect(array, axis):
    copies = jnp.broadcast_to(array, (lax.axis_size(axis) // 2, *array.shape))
    blocks = lax.all_to_all(
        copies, axis, 0, 0, tiled=True, axis_index_groups=core_groups(axis)
    )
    return with_sibling(blocks, axis)


def in_order(blocks, dim):
    shape = list(blocks.shape[1:])
    shape[dim] *= blocks.shape[0]
    return jnp.moveaxis(blocks, 0, dim).reshape(shape)


def sent_to_all(array, axis):
    copies = jnp.broadcast_to(array, (lax.axis_size(axis), *array.shape))
    return lax.all_to_all(copies, axis, split_axis=0, concat_axis=0, tiled=True)


def collect(array, axis, dim):
    return in_order(sent_to_all(array, axis), dim)


def turned_gather(arrays, axis, dims):
    turned = [jnp.moveaxis(a, dim, 0) for a, dim in zip(arrays, dims)]
    widths = [t[0].size for t in turned]
    both = jnp.concatenate([t.reshape(-1, w) for t, w in zip(turned, widths)], axis=1)
    out = lax.all_gather(both, axis, axis=0, tiled=True)
    blocks = jnp.split(out, [sum(widths[:k]) for k in range(1, len(widths))], axis=1)
    return tuple(
        (
            jnp.moveaxis(b.reshape(-1, *t.shape[1:]), 0, dim)
            for b, t, dim in zip(blocks, turned, dims)
        )
    )


def rms_scale(values, gain):
    values = values.astype(jnp.float32)
    inverse = lax.rsqrt(jnp.mean(values * values, axis=-1, keepdims=True) + EPS)
    return values * inverse * gain


def per_device(
    residual_in,
    attention_out,
    out_weight,
    post_gain,
    router_weight,
    expert_ids,
    expert_slot,
    expert_gate_up,
    expert_down,
    shared_gate_up,
    shared_down,
    final_gain,
):
    rows = residual_in.shape[0]
    width = residual_in.shape[1]
    experts = router_weight.shape[1]
    choose = expert_ids.shape[1]
    groups = lax.axis_size("dp")
    me = lax.axis_index("dp")
    capacity = max(2, min(rows, 2 * rows * choose // experts))
    proj_cols = jnp.dot(
        in_order(pair_collect(attention_out, "dp"), 0), out_weight, preferred_element_type=jnp.float32
    ).astype(jnp.bfloat16)
    proj = lax.all_to_all(proj_cols, "dp", split_axis=0, concat_axis=1, tiled=True)
    resid = (residual_in.astype(jnp.float32) + proj.astype(jnp.float32)).astype(jnp.bfloat16)
    normed = rms_scale(resid, post_gain).astype(jnp.bfloat16)
    logits = jnp.dot(normed, router_weight, preferred_element_type=jnp.float32)
    expert_range = jnp.arange(experts, dtype=jnp.int32)
    picked = expert_ids[:, :, None] == expert_range[None, None, :]
    chosen = jnp.sum(jnp.where(picked, logits[:, None, :], 0.0), axis=2)
    raised = jnp.exp(chosen)
    gates = raised / jnp.sum(raised, axis=1, keepdims=True)
    slots = jnp.sum(jnp.where(picked, expert_slot[None, None, :], 0), axis=2).reshape(-1)
    marked = (slots[:, None] == expert_range[None, :]).astype(jnp.int32)
    before = jnp.cumsum(marked, axis=0) - marked
    position = jnp.sum(before * marked, axis=1)
    target = slots * capacity + position
    placed = target[:, None] == jnp.arange(experts * capacity, dtype=jnp.int32)[None, :]
    select = jnp.any(placed.reshape(rows, choose, experts * capacity), axis=1).astype(jnp.bfloat16)
    outgoing = jnp.einsum("rs,rd->sd", select, normed, preferred_element_type=jnp.float32)
    outgoing = outgoing.astype(jnp.bfloat16).reshape(experts, capacity, width)
    hidden_units = expert_down.shape[1]
    weights_part = jnp.concatenate([expert_gate_up[0], expert_down[0].T], axis=1)
    own_blocks = lax.all_gather(
        weights_part, "dp", axis=0, tiled=True, axis_index_groups=core_groups("dp")
    )
    core = me % 2
    received = lax.all_to_all(outgoing, "expert", split_axis=0, concat_axis=0, tiled=True)
    sources, count, _ = received.shape
    flat = received.reshape(sources * count, width)
    sib_blocks = lax.ppermute(own_blocks, "dp", [(i, i ^ 1) for i in range(groups)])
    split = flat.reshape(flat.shape[0], groups // 2, 2, -1)
    own_cols = lax.dynamic_index_in_dim(split, core, axis=2, keepdims=False)
    sib_cols = lax.dynamic_index_in_dim(split, 1 - core, axis=2, keepdims=False)
    gate_up_width = 2 * hidden_units
    both = jnp.dot(
        own_cols.reshape(flat.shape[0], -1),
        own_blocks[:, :gate_up_width],
        preferred_element_type=jnp.float32,
    ) + jnp.dot(
        sib_cols.reshape(flat.shape[0], -1),
        sib_blocks[:, :gate_up_width],
        preferred_element_type=jnp.float32,
    )
    active = (jax.nn.silu(both[:, :hidden_units]) * both[:, hidden_units:]).astype(jnp.bfloat16)

    def down(blocks):
        part = lax.dot_general(
            active, blocks[:, gate_up_width:], (((1,), (1,)), ((), ())),
            preferred_element_type=jnp.float32,
        ).astype(jnp.bfloat16)
        return part.reshape(part.shape[0], groups // 2, -1)

    pair = jnp.stack([down(own_blocks), down(sib_blocks)], axis=2)
    pair = jnp.where(core == 0, pair, jnp.flip(pair, axis=2))
    result = pair.reshape(pair.shape[0], -1)
    result = result.reshape(sources, count, width)
    returned = lax.all_to_all(result, "expert", split_axis=0, concat_axis=0, tiled=True)
    shared_units = shared_gate_up.shape[2]
    shared_pair = shared_gate_up.reshape(width, 2 * shared_units)
    normed_shared = normed + (own_blocks[0, 0] * 0 + outgoing[0, 0, 0] * 0).astype(normed.dtype)
    both = jnp.dot(
        lax.all_gather(normed_shared, "dp", axis=0, tiled=True),
        shared_pair,
        preferred_element_type=jnp.float32,
    )
    shared_hidden = (jax.nn.silu(both[:, :shared_units]) * both[:, shared_units:]).astype(
        jnp.bfloat16
    )
    out_cols = jnp.dot(
        lax.all_gather(shared_hidden, "dp", axis=1, tiled=True),
        shared_down,
        preferred_element_type=jnp.float32,
    )
    shared_out = lax.all_to_all(
        out_cols.astype(jnp.bfloat16), "dp", split_axis=0, concat_axis=1, tiled=True
    ).astype(jnp.float32)
    weighted = jnp.sum(
        placed.reshape(rows, choose, experts * capacity) * gates[:, :, None], axis=1
    )
    routed = jnp.dot(
        weighted,
        returned.reshape(experts * capacity, width).astype(jnp.float32),
        precision=lax.Precision.HIGHEST,
        preferred_element_type=jnp.float32,
    )
    total = resid.astype(jnp.float32) + routed + shared_out
    return rms_scale(total, final_gain).astype(jnp.bfloat16)


def solution(mesh):
    in_specs = (
        P(("dp", "expert"), None),
        P(("dp", "expert"), None),
        P(None, "dp"),
        P(),
        P(),
        P(("dp", "expert"), None),
        P(),
        P("expert", "dp", None),
        P("expert", None, "dp"),
        P(None, None, "dp"),
        P(None, "dp"),
        P(),
    )
    out_specs = P(("dp", "expert"), None)
    return jax.shard_map(
        per_device, mesh=mesh, in_specs=in_specs, out_specs=out_specs, check_vma=False
    )
```

```python
import jax
import jax.numpy as jnp
from jax import lax
from jax.sharding import PartitionSpec as P

EPS = 1e-06


def core_groups(axis):
    n = lax.axis_size(axis)
    return [list(range(0, n, 2)), list(range(1, n, 2))]


def with_sibling(blocks, axis):
    other = lax.ppermute(blocks, axis, [(i, i ^ 1) for i in range(lax.axis_size(axis))])
    pair = jnp.stack([blocks, other], axis=1)
    pair = jnp.where(lax.axis_index(axis) % 2 == 0, pair, jnp.flip(pair, axis=1))
    return pair.reshape(-1, *blocks.shape[1:])


def pair_gather(array, axis):
    blocks = lax.all_gather(array, axis, axis=0, axis_index_groups=core_groups(axis))
    return with_sibling(blocks, axis)


def pair_collect(array, axis):
    copies = jnp.broadcast_to(array, (lax.axis_size(axis) // 2, *array.shape))
    blocks = lax.all_to_all(
        copies, axis, 0, 0, tiled=True, axis_index_groups=core_groups(axis)
    )
    return with_sibling(blocks, axis)


def in_order(blocks, dim):
    shape = list(blocks.shape[1:])
    shape[dim] *= blocks.shape[0]
    return jnp.moveaxis(blocks, 0, dim).reshape(shape)


def sent_to_all(array, axis):
    copies = jnp.broadcast_to(array, (lax.axis_size(axis), *array.shape))
    return lax.all_to_all(copies, axis, split_axis=0, concat_axis=0, tiled=True)


def collect(array, axis, dim):
    return in_order(sent_to_all(array, axis), dim)


def turned_gather(arrays, axis, dims):
    turned = [jnp.moveaxis(a, dim, 0) for a, dim in zip(arrays, dims)]
    widths = [t[0].size for t in turned]
    both = jnp.concatenate([t.reshape(-1, w) for t, w in zip(turned, widths)], axis=1)
    out = lax.all_gather(both, axis, axis=0, tiled=True)
    blocks = jnp.split(out, [sum(widths[:k]) for k in range(1, len(widths))], axis=1)
    return tuple(
        (
            jnp.moveaxis(b.reshape(-1, *t.shape[1:]), 0, dim)
            for b, t, dim in zip(blocks, turned, dims)
        )
    )


def rms_scale(values, gain):
    values = values.astype(jnp.float32)
    inverse = lax.rsqrt(jnp.mean(values * values, axis=-1, keepdims=True) + EPS)
    return values * inverse * gain


def per_device(
    residual_in,
    attention_out,
    out_weight,
    post_gain,
    router_weight,
    expert_ids,
    expert_slot,
    expert_gate_up,
    expert_down,
    shared_gate_up,
    shared_down,
    final_gain,
):
    rows = residual_in.shape[0]
    width = residual_in.shape[1]
    experts = router_weight.shape[1]
    choose = expert_ids.shape[1]
    capacity = max(2, min(rows, 2 * rows * choose // experts))
    proj_cols = jnp.dot(
        in_order(pair_collect(attention_out, "dp"), 0), out_weight, preferred_element_type=jnp.float32
    ).astype(jnp.bfloat16)
    proj = lax.all_to_all(proj_cols, "dp", split_axis=0, concat_axis=1, tiled=True)
    resid = (residual_in.astype(jnp.float32) + proj.astype(jnp.float32)).astype(jnp.bfloat16)
    normed = rms_scale(resid, post_gain).astype(jnp.bfloat16)
    logits = jnp.dot(normed, router_weight, preferred_element_type=jnp.float32)
    expert_range = jnp.arange(experts, dtype=jnp.int32)
    picked = expert_ids[:, :, None] == expert_range[None, None, :]
    chosen = jnp.sum(jnp.where(picked, logits[:, None, :], 0.0), axis=2)
    raised = jnp.exp(chosen)
    gates = raised / jnp.sum(raised, axis=1, keepdims=True)
    slots = jnp.sum(jnp.where(picked, expert_slot[None, None, :], 0), axis=2).reshape(-1)
    marked = (slots[:, None] == expert_range[None, :]).astype(jnp.int32)
    before = jnp.cumsum(marked, axis=0) - marked
    position = jnp.sum(before * marked, axis=1)
    target = slots * capacity + position
    placed = target[:, None] == jnp.arange(experts * capacity, dtype=jnp.int32)[None, :]
    select = jnp.any(placed.reshape(rows, choose, experts * capacity), axis=1).astype(jnp.bfloat16)
    outgoing = jnp.einsum("rs,rd->sd", select, normed, preferred_element_type=jnp.float32)
    outgoing = outgoing.astype(jnp.bfloat16).reshape(experts, capacity, width)
    gate_up_all, down_all = turned_gather((expert_gate_up, expert_down), "dp", (1, 2))
    gate_up_full = gate_up_all[0]
    down_full = down_all[0]
    hidden_units = gate_up_full.shape[1] // 2
    received = lax.all_to_all(outgoing, "expert", split_axis=0, concat_axis=0, tiled=True)
    sources, count, _ = received.shape
    flat = received.reshape(sources * count, width)
    both = jnp.dot(flat, gate_up_full, preferred_element_type=jnp.float32)
    active = (jax.nn.silu(both[:, :hidden_units]) * both[:, hidden_units:]).astype(jnp.bfloat16)
    result = jnp.dot(active, down_full, preferred_element_type=jnp.float32).astype(jnp.bfloat16)
    result = result.reshape(sources, count, width)
    returned = lax.all_to_all(result, "expert", split_axis=0, concat_axis=0, tiled=True)
    shared_units = shared_gate_up.shape[2]
    shared_pair = shared_gate_up.reshape(width, 2 * shared_units)
    normed_shared = normed + (gate_up_full[0, 0] * 0 + outgoing[0, 0, 0] * 0).astype(normed.dtype)
    both = jnp.dot(
        in_order(pair_gather(normed_shared, "dp"), 0),
        shared_pair,
        preferred_element_type=jnp.float32,
    )
    shared_hidden = (jax.nn.silu(both[:, :shared_units]) * both[:, shared_units:]).astype(
        jnp.bfloat16
    )
    out_cols = jnp.dot(
        in_order(pair_gather(shared_hidden, "dp"), 1),
        shared_down,
        preferred_element_type=jnp.float32,
    )
    shared_out = lax.all_to_all(
        out_cols.astype(jnp.bfloat16), "dp", split_axis=0, concat_axis=1, tiled=True
    ).astype(jnp.float32)
    weighted = jnp.sum(
        placed.reshape(rows, choose, experts * capacity) * gates[:, :, None], axis=1
    )
    routed = jnp.dot(
        weighted,
        returned.reshape(experts * capacity, width).astype(jnp.float32),
        precision=lax.Precision.HIGHEST,
        preferred_element_type=jnp.float32,
    )
    total = resid.astype(jnp.float32) + routed + shared_out
    return rms_scale(total, final_gain).astype(jnp.bfloat16)


def solution(mesh):
    in_specs = (
        P(("dp", "expert"), None),
        P(("dp", "expert"), None),
        P(None, "dp"),
        P(),
        P(),
        P(("dp", "expert"), None),
        P(),
        P("expert", "dp", None),
        P("expert", None, "dp"),
        P(None, None, "dp"),
        P(None, "dp"),
        P(),
    )
    out_specs = P(("dp", "expert"), None)
    return jax.shard_map(
        per_device, mesh=mesh, in_specs=in_specs, out_specs=out_specs, check_vma=False
    )
```

```python
import jax
import jax.numpy as jnp
from jax import lax
from jax.sharding import PartitionSpec as P

EPS = 1e-06


def core_groups(axis):
    n = lax.axis_size(axis)
    return [list(range(0, n, 2)), list(range(1, n, 2))]


def with_sibling(blocks, axis):
    other = lax.ppermute(blocks, axis, [(i, i ^ 1) for i in range(lax.axis_size(axis))])
    pair = jnp.stack([blocks, other], axis=1)
    pair = jnp.where(lax.axis_index(axis) % 2 == 0, pair, jnp.flip(pair, axis=1))
    return pair.reshape(-1, *blocks.shape[1:])


def pair_gather(array, axis):
    blocks = lax.all_gather(array, axis, axis=0, axis_index_groups=core_groups(axis))
    return with_sibling(blocks, axis)


def pair_collect(array, axis):
    copies = jnp.broadcast_to(array, (lax.axis_size(axis) // 2, *array.shape))
    blocks = lax.all_to_all(
        copies, axis, 0, 0, tiled=True, axis_index_groups=core_groups(axis)
    )
    return with_sibling(blocks, axis)


def in_order(blocks, dim):
    shape = list(blocks.shape[1:])
    shape[dim] *= blocks.shape[0]
    return jnp.moveaxis(blocks, 0, dim).reshape(shape)


def sent_to_all(array, axis):
    copies = jnp.broadcast_to(array, (lax.axis_size(axis), *array.shape))
    return lax.all_to_all(copies, axis, split_axis=0, concat_axis=0, tiled=True)


def collect(array, axis, dim):
    return in_order(sent_to_all(array, axis), dim)


def turned_gather(arrays, axis, dims):
    turned = [jnp.moveaxis(a, dim, 0) for a, dim in zip(arrays, dims)]
    widths = [t[0].size for t in turned]
    both = jnp.concatenate([t.reshape(-1, w) for t, w in zip(turned, widths)], axis=1)
    out = lax.all_gather(both, axis, axis=0, tiled=True)
    blocks = jnp.split(out, [sum(widths[:k]) for k in range(1, len(widths))], axis=1)
    return tuple(
        (
            jnp.moveaxis(b.reshape(-1, *t.shape[1:]), 0, dim)
            for b, t, dim in zip(blocks, turned, dims)
        )
    )


def rms_scale(values, gain):
    values = values.astype(jnp.float32)
    inverse = lax.rsqrt(jnp.mean(values * values, axis=-1, keepdims=True) + EPS)
    return values * inverse * gain


def per_device(
    residual_in,
    attention_out,
    out_weight,
    post_gain,
    router_weight,
    expert_ids,
    expert_slot,
    expert_gate_up,
    expert_down,
    shared_gate_up,
    shared_down,
    final_gain,
):
    rows = residual_in.shape[0]
    width = residual_in.shape[1]
    experts = router_weight.shape[1]
    choose = expert_ids.shape[1]
    capacity = max(2, min(rows, 2 * rows * choose // experts))
    proj_cols = jnp.dot(
        in_order(pair_collect(attention_out, "dp"), 0), out_weight, preferred_element_type=jnp.float32
    ).astype(jnp.bfloat16)
    proj = lax.all_to_all(proj_cols, "dp", split_axis=0, concat_axis=1, tiled=True)
    resid = (residual_in.astype(jnp.float32) + proj.astype(jnp.float32)).astype(jnp.bfloat16)
    normed = rms_scale(resid, post_gain).astype(jnp.bfloat16)
    logits = jnp.dot(normed, router_weight, preferred_element_type=jnp.float32)
    expert_range = jnp.arange(experts, dtype=jnp.int32)
    picked = expert_ids[:, :, None] == expert_range[None, None, :]
    chosen = jnp.sum(jnp.where(picked, logits[:, None, :], 0.0), axis=2)
    raised = jnp.exp(chosen)
    gates = raised / jnp.sum(raised, axis=1, keepdims=True)
    slots = jnp.sum(jnp.where(picked, expert_slot[None, None, :], 0), axis=2).reshape(-1)
    marked = (slots[:, None] == expert_range[None, :]).astype(jnp.int32)
    before = jnp.cumsum(marked, axis=0) - marked
    position = jnp.sum(before * marked, axis=1)
    target = slots * capacity + position
    placed = target[:, None] == jnp.arange(experts * capacity, dtype=jnp.int32)[None, :]
    select = jnp.any(placed.reshape(rows, choose, experts * capacity), axis=1).astype(jnp.bfloat16)
    outgoing = jnp.einsum("rs,rd->sd", select, normed, preferred_element_type=jnp.float32)
    outgoing = outgoing.astype(jnp.bfloat16).reshape(experts, capacity, width)
    gate_up_all, down_all = turned_gather((expert_gate_up, expert_down), "dp", (1, 2))
    gate_up_full = gate_up_all[0]
    down_full = down_all[0]
    hidden_units = gate_up_full.shape[1] // 2
    received = lax.all_to_all(outgoing, "expert", split_axis=0, concat_axis=0, tiled=True)
    sources, count, _ = received.shape
    flat = received.reshape(sources * count, width)
    both = jnp.dot(flat, gate_up_full, preferred_element_type=jnp.float32)
    active = (jax.nn.silu(both[:, :hidden_units]) * both[:, hidden_units:]).astype(jnp.bfloat16)
    result = jnp.dot(active, down_full, preferred_element_type=jnp.float32).astype(jnp.bfloat16)
    result = result.reshape(sources, count, width)
    returned = lax.all_to_all(result, "expert", split_axis=0, concat_axis=0, tiled=True)
    shared_units = shared_gate_up.shape[2]
    shared_pair = shared_gate_up.reshape(width, 2 * shared_units)
    normed_shared = normed + (gate_up_full[0, 0] * 0 + outgoing[0, 0, 0] * 0).astype(normed.dtype)
    both = jnp.dot(
        in_order(pair_gather(normed_shared, "dp"), 0),
        shared_pair,
        preferred_element_type=jnp.float32,
    )
    shared_hidden = (jax.nn.silu(both[:, :shared_units]) * both[:, shared_units:]).astype(
        jnp.bfloat16
    )
    groups_dp = lax.axis_size("dp")
    down_blocks = shared_down.reshape(groups_dp, shared_units, -1)
    down_rows = lax.all_to_all(down_blocks, "dp", 0, 0, tiled=True)
    down_rows = in_order(down_rows, 1)
    partial = jnp.dot(shared_hidden, down_rows, preferred_element_type=jnp.float32)
    partial = partial + (result[0, 0, 0] * 0).astype(partial.dtype)
    shared_out = lax.psum_scatter(partial, "dp", scatter_dimension=0, tiled=True)
    weighted = jnp.sum(
        placed.reshape(rows, choose, experts * capacity) * gates[:, :, None], axis=1
    )
    routed = jnp.dot(
        weighted,
        returned.reshape(experts * capacity, width).astype(jnp.float32),
        precision=lax.Precision.HIGHEST,
        preferred_element_type=jnp.float32,
    )
    total = resid.astype(jnp.float32) + routed + shared_out
    return rms_scale(total, final_gain).astype(jnp.bfloat16)


def solution(mesh):
    in_specs = (
        P(("dp", "expert"), None),
        P(("dp", "expert"), None),
        P(None, "dp"),
        P(),
        P(),
        P(("dp", "expert"), None),
        P(),
        P("expert", "dp", None),
        P("expert", None, "dp"),
        P(None, None, "dp"),
        P(None, "dp"),
        P(),
    )
    out_specs = P(("dp", "expert"), None)
    return jax.shard_map(
        per_device, mesh=mesh, in_specs=in_specs, out_specs=out_specs, check_vma=False
    )
```

```python
import jax
import jax.numpy as jnp
from jax import lax
from jax.sharding import PartitionSpec as P

EPS = 1e-06


def core_groups(axis):
    n = lax.axis_size(axis)
    return [list(range(0, n, 2)), list(range(1, n, 2))]


def with_sibling(blocks, axis):
    other = lax.ppermute(blocks, axis, [(i, i ^ 1) for i in range(lax.axis_size(axis))])
    pair = jnp.stack([blocks, other], axis=1)
    pair = jnp.where(lax.axis_index(axis) % 2 == 0, pair, jnp.flip(pair, axis=1))
    return pair.reshape(-1, *blocks.shape[1:])


def pair_gather(array, axis):
    blocks = lax.all_gather(array, axis, axis=0, axis_index_groups=core_groups(axis))
    return with_sibling(blocks, axis)


def pair_collect(array, axis):
    copies = jnp.broadcast_to(array, (lax.axis_size(axis) // 2, *array.shape))
    blocks = lax.all_to_all(
        copies, axis, 0, 0, tiled=True, axis_index_groups=core_groups(axis)
    )
    return with_sibling(blocks, axis)


def in_order(blocks, dim):
    shape = list(blocks.shape[1:])
    shape[dim] *= blocks.shape[0]
    return jnp.moveaxis(blocks, 0, dim).reshape(shape)


def sent_to_all(array, axis):
    copies = jnp.broadcast_to(array, (lax.axis_size(axis), *array.shape))
    return lax.all_to_all(copies, axis, split_axis=0, concat_axis=0, tiled=True)


def collect(array, axis, dim):
    return in_order(sent_to_all(array, axis), dim)


def turned_gather(arrays, axis, dims):
    turned = [jnp.moveaxis(a, dim, 0) for a, dim in zip(arrays, dims)]
    widths = [t[0].size for t in turned]
    both = jnp.concatenate([t.reshape(-1, w) for t, w in zip(turned, widths)], axis=1)
    out = lax.all_gather(both, axis, axis=0, tiled=True)
    blocks = jnp.split(out, [sum(widths[:k]) for k in range(1, len(widths))], axis=1)
    return tuple(
        (
            jnp.moveaxis(b.reshape(-1, *t.shape[1:]), 0, dim)
            for b, t, dim in zip(blocks, turned, dims)
        )
    )


def rms_scale(values, gain):
    values = values.astype(jnp.float32)
    inverse = lax.rsqrt(jnp.mean(values * values, axis=-1, keepdims=True) + EPS)
    return values * inverse * gain


def per_device(
    residual_in,
    attention_out,
    out_weight,
    post_gain,
    router_weight,
    expert_ids,
    expert_slot,
    expert_gate_up,
    expert_down,
    shared_gate_up,
    shared_down,
    final_gain,
):
    rows = residual_in.shape[0]
    width = residual_in.shape[1]
    experts = router_weight.shape[1]
    choose = expert_ids.shape[1]
    capacity = max(2, min(rows, 2 * rows * choose // experts))
    proj_cols = jnp.dot(
        in_order(pair_collect(attention_out, "dp"), 0), out_weight, preferred_element_type=jnp.float32
    ).astype(jnp.bfloat16)
    proj = lax.all_to_all(proj_cols, "dp", split_axis=0, concat_axis=1, tiled=True)
    resid = (residual_in.astype(jnp.float32) + proj.astype(jnp.float32)).astype(jnp.bfloat16)
    normed = rms_scale(resid, post_gain).astype(jnp.bfloat16)
    logits = jnp.dot(normed, router_weight, preferred_element_type=jnp.float32)
    expert_range = jnp.arange(experts, dtype=jnp.int32)
    ids = expert_ids + (proj_cols[0, 0] * 0).astype(expert_ids.dtype)
    picked = ids[:, :, None] == expert_range[None, None, :]
    chosen = jnp.sum(jnp.where(picked, logits[:, None, :], 0.0), axis=2)
    raised = jnp.exp(chosen)
    gates = raised / jnp.sum(raised, axis=1, keepdims=True)
    slots = jnp.sum(jnp.where(picked, expert_slot[None, None, :], 0), axis=2).reshape(-1)
    marked = (slots[:, None] == expert_range[None, :]).astype(jnp.int32)
    before = jnp.cumsum(marked, axis=0) - marked
    position = jnp.sum(before * marked, axis=1)
    target = slots * capacity + position
    placed = target[:, None] == jnp.arange(experts * capacity, dtype=jnp.int32)[None, :]
    select = jnp.any(placed.reshape(rows, choose, experts * capacity), axis=1).astype(jnp.bfloat16)
    outgoing = jnp.einsum("rs,rd->sd", select, normed, preferred_element_type=jnp.float32)
    outgoing = outgoing.astype(jnp.bfloat16).reshape(experts, capacity, width)
    gate_up_all, down_all = turned_gather((expert_gate_up, expert_down), "dp", (1, 2))
    gate_up_full = gate_up_all[0]
    down_full = down_all[0]
    hidden_units = gate_up_full.shape[1] // 2
    received = lax.all_to_all(outgoing, "expert", split_axis=0, concat_axis=0, tiled=True)
    sources, count, _ = received.shape
    flat = received.reshape(sources * count, width)
    both = jnp.dot(flat, gate_up_full, preferred_element_type=jnp.float32)
    active = (jax.nn.silu(both[:, :hidden_units]) * both[:, hidden_units:]).astype(jnp.bfloat16)
    result = jnp.dot(active, down_full, preferred_element_type=jnp.float32).astype(jnp.bfloat16)
    result = result.reshape(sources, count, width)
    returned = lax.all_to_all(result, "expert", split_axis=0, concat_axis=0, tiled=True)
    shared_units = shared_gate_up.shape[2]
    shared_pair = shared_gate_up.reshape(width, 2 * shared_units)
    normed_shared = normed + (gate_up_full[0, 0] * 0 + outgoing[0, 0, 0] * 0).astype(normed.dtype)
    both = jnp.dot(
        in_order(pair_gather(normed_shared, "dp"), 0),
        shared_pair,
        preferred_element_type=jnp.float32,
    )
    shared_hidden = (jax.nn.silu(both[:, :shared_units]) * both[:, shared_units:]).astype(
        jnp.bfloat16
    )
    out_cols = jnp.dot(
        in_order(pair_gather(shared_hidden, "dp"), 1),
        shared_down,
        preferred_element_type=jnp.float32,
    )
    shared_out = lax.all_to_all(
        out_cols.astype(jnp.bfloat16), "dp", split_axis=0, concat_axis=1, tiled=True
    ).astype(jnp.float32)
    weighted = jnp.sum(
        placed.reshape(rows, choose, experts * capacity) * gates[:, :, None], axis=1
    )
    routed = jnp.dot(
        weighted,
        returned.reshape(experts * capacity, width).astype(jnp.float32),
        precision=lax.Precision.HIGHEST,
        preferred_element_type=jnp.float32,
    )
    total = resid.astype(jnp.float32) + routed + shared_out
    return rms_scale(total, final_gain).astype(jnp.bfloat16)


def solution(mesh):
    in_specs = (
        P(("dp", "expert"), None),
        P(("dp", "expert"), None),
        P(None, "dp"),
        P(),
        P(),
        P(("dp", "expert"), None),
        P(),
        P("expert", "dp", None),
        P("expert", None, "dp"),
        P(None, None, "dp"),
        P(None, "dp"),
        P(),
    )
    out_specs = P(("dp", "expert"), None)
    return jax.shard_map(
        per_device, mesh=mesh, in_specs=in_specs, out_specs=out_specs, check_vma=False
    )
```

```python
import jax
import jax.numpy as jnp
from jax import lax
from jax.sharding import PartitionSpec as P

EPS = 1e-06


def core_groups(axis):
    n = lax.axis_size(axis)
    return [list(range(0, n, 2)), list(range(1, n, 2))]


def with_sibling(blocks, axis):
    other = lax.ppermute(blocks, axis, [(i, i ^ 1) for i in range(lax.axis_size(axis))])
    pair = jnp.stack([blocks, other], axis=1)
    pair = jnp.where(lax.axis_index(axis) % 2 == 0, pair, jnp.flip(pair, axis=1))
    return pair.reshape(-1, *blocks.shape[1:])


def pair_gather(array, axis):
    blocks = lax.all_gather(array, axis, axis=0, axis_index_groups=core_groups(axis))
    return with_sibling(blocks, axis)


def pair_collect(array, axis):
    copies = jnp.broadcast_to(array, (lax.axis_size(axis) // 2, *array.shape))
    blocks = lax.all_to_all(
        copies, axis, 0, 0, tiled=True, axis_index_groups=core_groups(axis)
    )
    return with_sibling(blocks, axis)


def in_order(blocks, dim):
    shape = list(blocks.shape[1:])
    shape[dim] *= blocks.shape[0]
    return jnp.moveaxis(blocks, 0, dim).reshape(shape)


def sent_to_all(array, axis):
    copies = jnp.broadcast_to(array, (lax.axis_size(axis), *array.shape))
    return lax.all_to_all(copies, axis, split_axis=0, concat_axis=0, tiled=True)


def collect(array, axis, dim):
    return in_order(sent_to_all(array, axis), dim)


def turned_gather(arrays, axis, dims):
    turned = [jnp.moveaxis(a, dim, 0) for a, dim in zip(arrays, dims)]
    widths = [t[0].size for t in turned]
    both = jnp.concatenate([t.reshape(-1, w) for t, w in zip(turned, widths)], axis=1)
    out = lax.all_gather(both, axis, axis=0, tiled=True)
    blocks = jnp.split(out, [sum(widths[:k]) for k in range(1, len(widths))], axis=1)
    return tuple(
        (
            jnp.moveaxis(b.reshape(-1, *t.shape[1:]), 0, dim)
            for b, t, dim in zip(blocks, turned, dims)
        )
    )


def rms_scale(values, gain):
    values = values.astype(jnp.float32)
    inverse = lax.rsqrt(jnp.mean(values * values, axis=-1, keepdims=True) + EPS)
    return values * inverse * gain


def per_device(
    residual_in,
    attention_out,
    out_weight,
    post_gain,
    router_weight,
    expert_ids,
    expert_slot,
    expert_gate_up,
    expert_down,
    shared_gate_up,
    shared_down,
    final_gain,
):
    rows = residual_in.shape[0]
    width = residual_in.shape[1]
    experts = router_weight.shape[1]
    choose = expert_ids.shape[1]
    capacity = max(2, min(rows, 2 * rows * choose // experts))
    proj_cols = jnp.dot(
        in_order(pair_collect(attention_out, "dp"), 0), out_weight, preferred_element_type=jnp.float32
    ).astype(jnp.bfloat16)
    proj = lax.all_to_all(proj_cols, "dp", split_axis=0, concat_axis=1, tiled=True)
    resid = (residual_in.astype(jnp.float32) + proj.astype(jnp.float32)).astype(jnp.bfloat16)
    normed = rms_scale(resid, post_gain).astype(jnp.bfloat16)
    logits = jnp.dot(normed, router_weight, preferred_element_type=jnp.float32)
    expert_range = jnp.arange(experts, dtype=jnp.int32)
    ids = expert_ids + (proj_cols[0, 0] * 0).astype(expert_ids.dtype)
    picked = ids[:, :, None] == expert_range[None, None, :]
    chosen = jnp.sum(jnp.where(picked, logits[:, None, :], 0.0), axis=2)
    raised = jnp.exp(chosen)
    gates = raised / jnp.sum(raised, axis=1, keepdims=True)
    slots = jnp.sum(jnp.where(picked, expert_slot[None, None, :], 0), axis=2).reshape(-1)
    marked = (slots[:, None] == expert_range[None, :]).astype(jnp.int32)
    before = jnp.cumsum(marked, axis=0) - marked
    position = jnp.sum(before * marked, axis=1)
    target = slots * capacity + position
    placed = target[:, None] == jnp.arange(experts * capacity, dtype=jnp.int32)[None, :]
    select = jnp.any(placed.reshape(rows, choose, experts * capacity), axis=1).astype(jnp.bfloat16)
    outgoing = jnp.einsum("rs,rd->sd", select, normed, preferred_element_type=jnp.float32)
    outgoing = outgoing.astype(jnp.bfloat16).reshape(experts, capacity, width)
    hidden_units = expert_down.shape[1]
    weights_part = jnp.concatenate([expert_gate_up[0], expert_down[0].T], axis=1)
    weights_full = lax.all_gather(weights_part, "dp", axis=0, tiled=True)
    gate_up_full = weights_full[:, : 2 * hidden_units]
    down_turned_full = weights_full[:, 2 * hidden_units :]
    received = lax.all_to_all(outgoing, "expert", split_axis=0, concat_axis=0, tiled=True)
    sources, count, _ = received.shape
    flat = received.reshape(sources * count, width)
    both = jnp.dot(flat, gate_up_full, preferred_element_type=jnp.float32)
    active = (jax.nn.silu(both[:, :hidden_units]) * both[:, hidden_units:]).astype(jnp.bfloat16)
    result = lax.dot_general(
        active, down_turned_full, (((1,), (1,)), ((), ())), preferred_element_type=jnp.float32
    ).astype(jnp.bfloat16)
    result = result.reshape(sources, count, width)
    returned = lax.all_to_all(result, "expert", split_axis=0, concat_axis=0, tiled=True)
    shared_units = shared_gate_up.shape[2]
    shared_pair = shared_gate_up.reshape(width, 2 * shared_units)
    normed_shared = normed + (weights_full[0, 0] * 0 + outgoing[0, 0, 0] * 0).astype(normed.dtype)
    both = jnp.dot(
        in_order(pair_gather(normed_shared, "dp"), 0),
        shared_pair,
        preferred_element_type=jnp.float32,
    )
    shared_hidden = (jax.nn.silu(both[:, :shared_units]) * both[:, shared_units:]).astype(
        jnp.bfloat16
    )
    out_cols = jnp.dot(
        in_order(pair_gather(shared_hidden, "dp"), 1),
        shared_down,
        preferred_element_type=jnp.float32,
    )
    shared_out = lax.all_to_all(
        out_cols.astype(jnp.bfloat16), "dp", split_axis=0, concat_axis=1, tiled=True
    ).astype(jnp.float32)
    weighted = jnp.sum(
        placed.reshape(rows, choose, experts * capacity) * gates[:, :, None], axis=1
    )
    routed = jnp.dot(
        weighted,
        returned.reshape(experts * capacity, width).astype(jnp.float32),
        precision=lax.Precision.HIGHEST,
        preferred_element_type=jnp.float32,
    )
    total = resid.astype(jnp.float32) + routed + shared_out
    return rms_scale(total, final_gain).astype(jnp.bfloat16)


def solution(mesh):
    in_specs = (
        P(("dp", "expert"), None),
        P(("dp", "expert"), None),
        P(None, "dp"),
        P(),
        P(),
        P(("dp", "expert"), None),
        P(),
        P("expert", "dp", None),
        P("expert", None, "dp"),
        P(None, None, "dp"),
        P(None, "dp"),
        P(),
    )
    out_specs = P(("dp", "expert"), None)
    return jax.shard_map(
        per_device, mesh=mesh, in_specs=in_specs, out_specs=out_specs, check_vma=False
    )
```

```python
import jax
import jax.numpy as jnp
from jax import lax
from jax.sharding import PartitionSpec as P

EPS = 1e-06


def core_groups(axis):
    n = lax.axis_size(axis)
    return [list(range(0, n, 2)), list(range(1, n, 2))]


def with_sibling(blocks, axis):
    other = lax.ppermute(blocks, axis, [(i, i ^ 1) for i in range(lax.axis_size(axis))])
    pair = jnp.stack([blocks, other], axis=1)
    pair = jnp.where(lax.axis_index(axis) % 2 == 0, pair, jnp.flip(pair, axis=1))
    return pair.reshape(-1, *blocks.shape[1:])


def pair_gather(array, axis):
    blocks = lax.all_gather(array, axis, axis=0, axis_index_groups=core_groups(axis))
    return with_sibling(blocks, axis)


def pair_collect(array, axis):
    copies = jnp.broadcast_to(array, (lax.axis_size(axis) // 2, *array.shape))
    blocks = lax.all_to_all(
        copies, axis, 0, 0, tiled=True, axis_index_groups=core_groups(axis)
    )
    return with_sibling(blocks, axis)


def in_order(blocks, dim):
    shape = list(blocks.shape[1:])
    shape[dim] *= blocks.shape[0]
    return jnp.moveaxis(blocks, 0, dim).reshape(shape)


def sent_to_all(array, axis):
    copies = jnp.broadcast_to(array, (lax.axis_size(axis), *array.shape))
    return lax.all_to_all(copies, axis, split_axis=0, concat_axis=0, tiled=True)


def collect(array, axis, dim):
    return in_order(sent_to_all(array, axis), dim)


def turned_gather(arrays, axis, dims):
    turned = [jnp.moveaxis(a, dim, 0) for a, dim in zip(arrays, dims)]
    widths = [t[0].size for t in turned]
    both = jnp.concatenate([t.reshape(-1, w) for t, w in zip(turned, widths)], axis=1)
    out = lax.all_gather(both, axis, axis=0, tiled=True)
    blocks = jnp.split(out, [sum(widths[:k]) for k in range(1, len(widths))], axis=1)
    return tuple(
        (
            jnp.moveaxis(b.reshape(-1, *t.shape[1:]), 0, dim)
            for b, t, dim in zip(blocks, turned, dims)
        )
    )


def rms_scale(values, gain):
    values = values.astype(jnp.float32)
    inverse = lax.rsqrt(jnp.mean(values * values, axis=-1, keepdims=True) + EPS)
    return values * inverse * gain


def per_device(
    residual_in,
    attention_out,
    out_weight,
    post_gain,
    router_weight,
    expert_ids,
    expert_slot,
    expert_gate_up,
    expert_down,
    shared_gate_up,
    shared_down,
    final_gain,
):
    rows = residual_in.shape[0]
    width = residual_in.shape[1]
    experts = router_weight.shape[1]
    choose = expert_ids.shape[1]
    capacity = max(2, min(rows, 2 * rows * choose // experts))
    proj_cols = jnp.dot(
        in_order(pair_collect(attention_out, "dp"), 0), out_weight, preferred_element_type=jnp.float32
    ).astype(jnp.bfloat16)
    proj = lax.all_to_all(proj_cols, "dp", split_axis=0, concat_axis=1, tiled=True)
    resid = (residual_in.astype(jnp.float32) + proj.astype(jnp.float32)).astype(jnp.bfloat16)
    normed = rms_scale(resid, post_gain).astype(jnp.bfloat16)
    logits = jnp.dot(normed, router_weight, preferred_element_type=jnp.float32)
    expert_range = jnp.arange(experts, dtype=jnp.int32)
    ids = expert_ids + (proj_cols[0, 0] * 0).astype(expert_ids.dtype)
    picked = ids[:, :, None] == expert_range[None, None, :]
    chosen = jnp.sum(jnp.where(picked, logits[:, None, :], 0.0), axis=2)
    raised = jnp.exp(chosen)
    gates = raised / jnp.sum(raised, axis=1, keepdims=True)
    slots = jnp.sum(jnp.where(picked, expert_slot[None, None, :], 0), axis=2).reshape(-1)
    marked = (slots[:, None] == expert_range[None, :]).astype(jnp.int32)
    before = jnp.cumsum(marked, axis=0) - marked
    position = jnp.sum(before * marked, axis=1)
    target = slots * capacity + position
    placed = target[:, None] == jnp.arange(experts * capacity, dtype=jnp.int32)[None, :]
    select = jnp.any(placed.reshape(rows, choose, experts * capacity), axis=1).astype(jnp.bfloat16)
    outgoing = jnp.einsum("rs,rd->sd", select, normed, preferred_element_type=jnp.float32)
    outgoing = outgoing.astype(jnp.bfloat16).reshape(experts, capacity, width)
    gate_up_all, down_all = turned_gather((expert_gate_up, expert_down), "dp", (1, 2))
    gate_up_full = gate_up_all[0]
    down_full = down_all[0]
    hidden_units = gate_up_full.shape[1] // 2
    received = lax.all_to_all(outgoing, "expert", split_axis=0, concat_axis=0, tiled=True)
    sources, count, _ = received.shape
    flat = received.reshape(sources * count, width)
    both = jnp.dot(flat, gate_up_full, preferred_element_type=jnp.float32)
    active = (jax.nn.silu(both[:, :hidden_units]) * both[:, hidden_units:]).astype(jnp.bfloat16)
    result = jnp.dot(active, down_full, preferred_element_type=jnp.float32).astype(jnp.bfloat16)
    result = result.reshape(sources, count, width)
    returned = lax.all_to_all(result, "expert", split_axis=0, concat_axis=0, tiled=True)
    shared_units = shared_gate_up.shape[2]
    shared_pair = shared_gate_up.reshape(width, 2 * shared_units)
    normed_shared = normed + (gate_up_full[0, 0] * 0 + outgoing[0, 0, 0] * 0).astype(normed.dtype)
    both = jnp.dot(
        in_order(pair_gather(normed_shared, "dp"), 0),
        shared_pair,
        preferred_element_type=jnp.float32,
    )
    shared_hidden = (jax.nn.silu(both[:, :shared_units]) * both[:, shared_units:]).astype(
        jnp.bfloat16
    )
    out_cols = jnp.dot(
        in_order(pair_gather(shared_hidden, "dp"), 1),
        shared_down,
        preferred_element_type=jnp.float32,
    )
    groups = lax.axis_size("dp")
    core = lax.axis_index("dp") % 2
    by_owner = out_cols.astype(jnp.bfloat16).reshape(groups // 2, 2, rows, -1)
    mine = lax.dynamic_index_in_dim(by_owner, core, axis=1, keepdims=False)
    theirs = lax.dynamic_index_in_dim(by_owner, 1 - core, axis=1, keepdims=False)
    swapped = lax.ppermute(theirs, "dp", [(i, i ^ 1) for i in range(groups)])
    blocks = jnp.where(
        core == 0, jnp.stack([mine, swapped], axis=2), jnp.stack([swapped, mine], axis=2)
    )
    blocks = lax.all_to_all(blocks, "dp", 0, 0, tiled=True, axis_index_groups=core_groups("dp"))
    shared_out = jnp.moveaxis(blocks, 0, 1).reshape(rows, -1).astype(jnp.float32)
    weighted = jnp.sum(
        placed.reshape(rows, choose, experts * capacity) * gates[:, :, None], axis=1
    )
    routed = jnp.dot(
        weighted,
        returned.reshape(experts * capacity, width).astype(jnp.float32),
        precision=lax.Precision.HIGHEST,
        preferred_element_type=jnp.float32,
    )
    total = resid.astype(jnp.float32) + routed + shared_out
    return rms_scale(total, final_gain).astype(jnp.bfloat16)


def solution(mesh):
    in_specs = (
        P(("dp", "expert"), None),
        P(("dp", "expert"), None),
        P(None, "dp"),
        P(),
        P(),
        P(("dp", "expert"), None),
        P(),
        P("expert", "dp", None),
        P("expert", None, "dp"),
        P(None, None, "dp"),
        P(None, "dp"),
        P(),
    )
    out_specs = P(("dp", "expert"), None)
    return jax.shard_map(
        per_device, mesh=mesh, in_specs=in_specs, out_specs=out_specs, check_vma=False
    )
```
